128 devices in a mesh: dp: 4 (over y), blk: 32 (over z, x, core).
Axes of the slice: x: 4, y: 4, z: 4, core: 2. Of those that a mesh axis runs over, the one named last changes fastest.
Arguments:
- queries: bfloat16 [32768, 1664], P(('dp', 'blk')), parts along dimension 0, as said below
- keys: bfloat16 [32768, 1664], P(('dp', 'blk')), parts along dimension 0, as said below
- values: bfloat16 [32768, 1664], P(('dp', 'blk')), parts along dimension 0, may hold values from -6 to 6
- residual_in: bfloat16 [32768, 1664], P(('dp', 'blk')), parts along dimension 0, as said below
- out_proj: bfloat16 [1664, 1664], replicated, may hold values from -0.15625 to 0.15625
- ln_gain: float32 [1664], replicated, may hold values from 0.1 to 1.9
- merge_proj: bfloat16 [6656, 4096], P('blk'), as said below
- out_gain: float32 [4096], replicated, may hold values from 0.1 to 1.9
- image_rows: int32 [64], P('dp'), parts along dimension 0, may hold values from 1 to 384, 2048 in all
- owners: int32 [8192, 1], P(('dp', 'blk')), parts along dimension 0, may hold values from 0 to 31; in each aligned block of 64 rows (0 to 63, 64 to 127, ...) at most 4 rows name the same one
Outputs:
- delivered: bfloat16 [16384, 4096], P(('dp', 'blk')), parts along dimension 0
The draws below stay inside these ranges and needn't reach their ends.
There are 4 independent parts, one for each index of `dp`. The reference program is written for one: setup_inputs(seed, part) draws one part's arguments, and reference() takes and returns one part's arrays. A program takes and returns all parts, laid end to end along the dimension named above; an argument that names none is the same for every part. Nothing has to cross between parts.
Inputs may be any that keep to these rules, and one draw needn't show every extreme that they name: `image_rows`: images lie end to end; their merged rows sum to 2048, and one image has exactly the most. `owners`: among the merged rows of one block no owner is named more than 4 times. `queries`: Real-valued; no structure is promised. `keys`: Real-valued; no structure is promised. `residual_in`: Real-valued; no structure is promised. `merge_proj`: Real-valued; no structure is promised.
All inputs are finite; a program needn't handle non-finite values.
Results may differ from the reference program's by a relative error of at most 0.017.
Values may be sent and summed in bfloat16 or wider, within the bound.
No kernel may reach another device: no remote copies, remote signals or barrier semaphores. Data moves between devices by JAX's collectives and lax.ppermute only.
A program may use at most 128 MiB of HBM per device.

```python
import math
import jax
import jax.numpy as jnp
import numpy as np
from jax import lax

D = 1664
HEADS = 16
HDIM = 104
OUTW = 4096
TOK_DEV = 256
TOKENS = 8192
MERGED = 6656
MROWS = 2048
MROW_DEV = 64
FEAT_DEV = 208
NIMG = 16
REACH = 6
CAP = 4
N_BLK = 32


def direction():
    place = jnp.arange(D, dtype=jnp.int32)
    return (1 - 2 * ((place * place + 3 * place) // 7 % 2)).astype(jnp.float32)


def query_base(key):
    return jax.random.normal(jax.random.fold_in(key, 1), (TOKENS, D), jnp.float32)


def far_partners(key):
    base = query_base(key)
    place = jnp.arange(TOKENS, dtype=jnp.int32)
    offset = REACH * TOK_DEV - 1 - jax.random.randint(jax.random.fold_in(key, 3), (TOKENS,), 0, TOK_DEV // 2)
    target = ((place + offset) % TOKENS).astype(jnp.int32)
    planted = jax.random.randint(jax.random.fold_in(key, 4), (TOKENS,), 0, 4) != 0
    strength = jax.random.uniform(jax.random.fold_in(key, 5), (TOKENS,), jnp.float32, 0.7, 1.2) * (8.0 / HDIM ** 0.5)
    factor = jnp.where(planted, strength, 0.0)
    return factor[:, None] * base[target]


def draw_queries(key, part):
    drawn = query_base(key)
    return jnp.clip(drawn, -24.0, 24.0).astype(jnp.bfloat16)


def draw_keys(key, part):
    drawn = jax.random.normal(jax.random.fold_in(key, 2), (TOKENS, D), jnp.float32) + far_partners(key)
    return jnp.clip(drawn, -24.0, 24.0).astype(jnp.bfloat16)


def draw_residual_in(key, part):
    blocks = TOKENS // TOK_DEV
    noise = jnp.clip(jax.random.normal(jax.random.fold_in(key, 21), (TOKENS, D), jnp.float32), -6.0, 6.0)
    block_strength = jax.random.uniform(jax.random.fold_in(key, 22), (blocks,), jnp.float32, 0.0, 0.6)
    row_sign = jnp.where(jax.random.randint(jax.random.fold_in(key, 23), (TOKENS // 4,), 0, 2) == 0, 1.0, -1.0)
    row_size = jax.random.uniform(jax.random.fold_in(key, 24), (TOKENS // 4,), jnp.float32, 0.5, 1.5)
    place = jnp.arange(TOKENS, dtype=jnp.int32)
    along = block_strength[place // TOK_DEV] * row_sign[place // 4] * row_size[place // 4]
    stream = 0.25 * noise + along[:, None] * direction()[None, :]
    return jnp.clip(stream, -2.5, 2.5).astype(jnp.bfloat16)


def draw_merge_proj(key, part):
    drawn = jnp.clip(jax.random.normal(jax.random.fold_in(key, 31), (MERGED, OUTW), jnp.float32), -6.0, 6.0)
    spread = 0.5
    column = jnp.clip(jax.random.normal(jax.random.fold_in(key, 32), (OUTW,), jnp.float32), -4.0, 4.0) * (spread / D)
    along = jnp.tile(direction(), 4)
    weight = drawn * MERGED ** (-0.5) + along[:, None] * column[None, :]
    return weight.astype(jnp.bfloat16)


def level_of(key, dims, pieces, low, top_value):
    level, own = 1.0, jax.random.fold_in(key, 6)
    for axis_at, blocks in pieces:
        draws = jnp.exp(jax.random.uniform(jax.random.fold_in(own, axis_at), (blocks,), jnp.float32, low / len(pieces), top_value / len(pieces)))
        level = level * jnp.repeat(draws, dims[axis_at] // blocks).reshape([-1 if axis == axis_at else 1 for axis in range(len(dims))])
    return level


def profile(count, total, most, skew):
    portions = [(1 << 20) // math.isqrt(standing ** skew) + 1 for standing in range(2, count + 1)]
    surplus, counts = total - most - (count - 1), [1] * (count - 1)
    while surplus > 0:
        free = [i for i in range(count - 1) if counts[i] < most]
        mass, budget = sum([portions[i] for i in free]), surplus
        for i in free:
            extra = min(most - counts[i], max(1, budget * portions[i] // mass), surplus)
            counts[i] = counts[i] + extra
            surplus = surplus - extra
    return np.array([most] + counts)


def ragged(own_key, number_of, total, limit, lean):
    if number_of == 2:
        one = jax.random.randint(own_key, (), max(1, total - limit), min(limit, total - 1) + 1)
        return jnp.stack([one, total - one])
    tallies = jnp.asarray(profile(number_of, total, limit, lean), jnp.int32)
    pairs = (number_of - 1) // 2
    source_of, sink = tallies[1:1 + 2 * pairs:2], tallies[2:2 + 2 * pairs:2]
    margin = jnp.minimum(source_of - 1, limit - sink)
    passed = jax.random.randint(jax.random.fold_in(own_key, 1), (pairs,), 0, 1 << 20) % (margin + 1)
    tallies = tallies.at[1:1 + 2 * pairs:2].set(source_of - passed).at[2:2 + 2 * pairs:2].set(sink + passed)
    return tallies[jax.random.permutation(jax.random.fold_in(own_key, 2), number_of)]


def deal_out(own_key, own, number, rows, number_of, top, reach, lean):
    order = jax.random.permutation(own_key, number_of)
    heavy_load, common = load_shares(number_of, rows * top, reach, lean, True), load_shares(number_of, rows * top, reach, lean, False)
    places = jnp.arange(number_of)

    def named(tallies, rotation):
        used = int((tallies > 0).sum())
        fixed = max(1, used // 4)
        passed = fixed + (places - fixed + rotation * (used - fixed)) % max(1, number_of - fixed)
        return jnp.zeros((number_of,), jnp.int32).at[order[jnp.where(places < fixed, places, passed)]].set(jnp.asarray(tallies, jnp.int32))

    tallies = jnp.where(number % 4 == 0, named(heavy_load, number // 4), named(common, number - number // 4 - 1))
    mixed = jax.random.permutation(jax.random.fold_in(own, 3), number_of)
    donor, taker = mixed[0:number_of // 2 * 2:2], mixed[1:number_of // 2 * 2:2]
    slack = jnp.minimum(tallies[donor] - 1, reach - tallies[taker]) // 2
    slack = jnp.where((donor == order[0]) | (taker == order[0]) | (tallies[taker] == 0), 0, jnp.maximum(slack, 0))
    passed = jax.random.randint(jax.random.fold_in(own, 4), (number_of // 2,), 0, 1 << 20) % (slack + 1)
    tallies = tallies.at[donor].add(-passed).at[taker].add(passed)
    members = jnp.searchsorted(jnp.cumsum(tallies), jnp.arange(rows * top), side="right").astype(jnp.int32)
    listing = members.reshape(top, rows).T
    listing = listing[jax.random.permutation(jax.random.fold_in(own, 1), rows)]
    rotation = jax.random.randint(jax.random.fold_in(own, 2), (rows, 1), 0, top)
    return jnp.take_along_axis(listing, (jnp.arange(top)[None, :] + rotation) % top, axis=1)


def load_shares(number_of, total, limit, slope, full):
    weights = [(1 << 20) // math.isqrt(rank ** slope) + 1 for rank in range(1, number_of + 1)]
    largest = limit if full else min(limit, max(-(-total // number_of), total * weights[0] // sum(weights)))
    least = 1 if total - largest >= number_of - 1 else 0
    counts, rest = [largest] + [least] * (number_of - 1), total - largest - least * (number_of - 1)
    while rest > 0:
        movable = [i for i in range(1, number_of) if counts[i] < largest] or [i for i in range(1, number_of) if counts[i] < limit]
        whole, budget = sum([weights[i] for i in movable]), rest
        for i in movable:
            more = min(limit - counts[i], max(1, budget * weights[i] // whole), rest)
            counts[i] = counts[i] + more
            rest = rest - more
    return np.array(counts)


def scatter_about(rng, extent, scale, reach, pieces=(), kind=jnp.bfloat16):
    result = jax.random.normal(rng, extent, jnp.float32) * scale
    if len(pieces) > 0:
        result = level_of(rng, extent, pieces, -0.22, 0.18) * result
    return jnp.clip(result, min=-reach, max=reach).astype(kind)


def setup_inputs(seed: int = 0, part: int = 0) -> dict:
    key_list = jax.random.split(jax.random.key(seed), 11)
    own_keys = jax.random.split(jax.random.fold_in(key_list[10], part), 11)
    queries = draw_queries(jax.random.fold_in(jax.random.fold_in(key_list[10], part), 71), part)
    keys = draw_keys(jax.random.fold_in(jax.random.fold_in(key_list[10], part), 71), part)
    values = scatter_about(own_keys[2], (TOKENS, D), 1.0, 6.0, ((0, 32),))
    residual_in = draw_residual_in(jax.random.fold_in(jax.random.fold_in(key_list[10], part), 71), part)
    out_proj = scatter_about(key_list[4], (D, D), D ** -0.5, 0.15625)
    ln_gain = jnp.clip(1.0 + 0.18 * jax.random.normal(key_list[5], (D,), jnp.float32), 0.1, 1.9)
    merge_proj = draw_merge_proj(jax.random.fold_in(key_list[10], 71), part)
    out_gain = jnp.clip(1.0 + 0.18 * jax.random.normal(key_list[7], (OUTW,), jnp.float32), 0.1, 1.9)
    image_rows = ragged(own_keys[8], NIMG, MROWS, REACH * MROW_DEV, 1).astype(jnp.int32)
    owners_keys = jax.random.split(jax.random.fold_in(own_keys[9], 1), MROWS // MROW_DEV)
    owners_turns = jax.random.permutation(jax.random.fold_in(own_keys[9], 3), MROWS // MROW_DEV)
    owners = jax.vmap(lambda own, number: deal_out(jax.random.fold_in(own_keys[9], 2), own, number, MROW_DEV, N_BLK, 1, CAP, 2))(owners_keys, owners_turns).reshape((MROWS, 1))
    return {"queries": queries, "keys": keys, "values": values, "residual_in": residual_in, "out_proj": out_proj, "ln_gain": ln_gain, "merge_proj": merge_proj, "out_gain": out_gain, "image_rows": image_rows, "owners": owners}


def image_of_rows(image_rows, count):
    ends = jnp.cumsum(image_rows)
    rows = jnp.arange(count, dtype=jnp.int32)
    return lax.optimization_barrier(jnp.sum((rows[:, None] >= ends[None, :]).astype(jnp.int32), axis=1)).astype(jnp.int32)

def reference(queries, keys, values, residual_in, out_proj, ln_gain, merge_proj, out_gain, image_rows, owners):
    row_image = image_of_rows(image_rows, MROWS)
    token_image = jnp.repeat(row_image, 4)
    scale = 1.0 / HDIM ** 0.5
    q_heads = queries.reshape(TOKENS, HEADS, HDIM).transpose(1, 0, 2)
    k_heads = keys.reshape(TOKENS, HEADS, HDIM).transpose(1, 0, 2)
    v_heads = values.reshape(TOKENS, HEADS, HDIM).transpose(1, 0, 2)
    same = token_image[:, None] == token_image[None, :]

    def one_head(parts):
        q_head, k_head, v_head = parts
        scores = jnp.dot(q_head, k_head.T, preferred_element_type=jnp.float32) * scale
        scores = jnp.where(same, scores, -jnp.inf)
        top = lax.optimization_barrier(jnp.max(scores, axis=1, keepdims=True))
        weights = jnp.exp(scores - top)
        total = lax.optimization_barrier(jnp.sum(weights, axis=1, keepdims=True))
        out = jnp.dot(weights.astype(jnp.bfloat16), v_head, preferred_element_type=jnp.float32) / total
        return out.astype(jnp.bfloat16)
    heads_out = lax.map(one_head, (q_heads, k_heads, v_heads))
    attended = heads_out.transpose(1, 0, 2).reshape(TOKENS, D)
    stream = residual_in.astype(jnp.float32) + jnp.dot(attended, out_proj, preferred_element_type=jnp.float32)
    mean = lax.optimization_barrier(jnp.mean(stream, axis=1, keepdims=True))
    centred = stream - mean
    var = lax.optimization_barrier(jnp.mean(centred * centred, axis=1, keepdims=True))
    normed = (centred * lax.rsqrt(var + 1e-06) * ln_gain[None, :]).astype(jnp.bfloat16)
    merged = normed.reshape(MROWS, MERGED)
    groups = merged.reshape(MROWS, N_BLK, FEAT_DEV).transpose(1, 0, 2)
    weight_groups = merge_proj.reshape(N_BLK, FEAT_DEV, OUTW)

    def add_group(carry, parts):
        feats, weight = parts
        partial_sum = jnp.dot(feats, weight, preferred_element_type=jnp.float32).astype(jnp.bfloat16)
        partial_sum = lax.optimization_barrier(partial_sum)
        return (carry + partial_sum.astype(jnp.float32), None)
    projected, unused = lax.scan(add_group, jnp.zeros((MROWS, OUTW), jnp.float32), (groups, weight_groups))
    row_squares = lax.optimization_barrier(jnp.sum(projected * projected, axis=1))
    member = (row_image[:, None] == jnp.arange(NIMG, dtype=jnp.int32)[None, :]).astype(jnp.float32)
    image_sums = lax.optimization_barrier(jnp.sum(member * row_squares[:, None], axis=0))
    image_mean = image_sums / (image_rows.astype(jnp.float32) * OUTW)
    row_scale = lax.rsqrt(image_mean + 1e-06)[row_image]
    scaled = (projected * row_scale[:, None] * out_gain[None, :]).astype(jnp.bfloat16)
    owner = owners[:, 0].astype(jnp.int32)
    source = (jnp.arange(MROWS, dtype=jnp.int32) // MROW_DEV).astype(jnp.int32)
    onehot = (owner[:, None] == jnp.arange(N_BLK, dtype=jnp.int32)[None, :]).astype(jnp.int32)
    running = jnp.cumsum(onehot.reshape(N_BLK, MROW_DEV, N_BLK), axis=1).reshape(MROWS, N_BLK)
    rank = lax.optimization_barrier(jnp.sum(running * onehot, axis=1)).astype(jnp.int32) - 1
    target = (owner * (N_BLK * CAP) + source * CAP + rank).astype(jnp.int32)
    delivered = jnp.zeros((N_BLK * N_BLK * CAP, OUTW), jnp.bfloat16).at[target].set(scaled)
    return delivered
```

```python
import jax
import jax.numpy as jnp
from jax import lax
from jax.sharding import PartitionSpec as P

HEADS = 16


def passed_along(value, axis, steps):
    count = lax.axis_size(axis)
    first, last = (max(0, -steps), min(count, count - steps))
    return lax.ppermute(value, axis, [(source, source + steps) for source in range(first, last)])


def layer_norm(stream, gain):
    mean = jnp.mean(stream, axis=1, keepdims=True)
    centred = stream - mean
    var = jnp.mean(centred * centred, axis=1, keepdims=True)
    return centred * lax.rsqrt(var + 1e-06) * gain[None, :]


def on_device(
    queries, keys, values, residual_in, out_proj, ln_gain, merge_proj, out_gain, image_rows, owners
):
    blocks = lax.axis_size("blk")
    me_index = lax.axis_index("blk")
    tok, width = queries.shape
    row_count = tok // 4
    heads = HEADS
    hdim = width // heads
    reach = min(6, (blocks - 1) // 2)
    scale = 1.0 / hdim**0.5
    ends = jnp.cumsum(image_rows)

    def row_images(source):
        rows = source * row_count + jnp.arange(row_count, dtype=jnp.int32)
        found = jnp.sum((rows[:, None] >= ends[None, :]).astype(jnp.int32), axis=1)
        inside = jnp.logical_and(source >= 0, source < blocks)
        return jnp.where(inside, found, -1)

    def token_images(source):
        return jnp.repeat(row_images(source), 4, total_repeat_length=tok)

    query_img = token_images(me_index)
    q_heads = queries.reshape(tok, heads, hdim)
    own_pair = jnp.stack([keys, values])

    def masked_scores(pair, key_img):
        k_heads = pair[0].reshape(-1, heads, hdim)
        scores = (
            jnp.einsum("qhd,khd->hqk", q_heads, k_heads, preferred_element_type=jnp.float32) * scale
        )
        return jnp.where(query_img[None, :, None] == key_img[None, None, :], scores, -jnp.inf)

    def weigh_values(weights, pair):
        v_heads = pair[1].reshape(-1, heads, hdim)
        return jnp.einsum(
            "hqk,khd->hqd",
            weights.astype(jnp.bfloat16),
            v_heads,
            preferred_element_type=jnp.float32,
        )

    def absorb(state, pair, key_img):

        def update(carry):
            running_max, running_sum, accum = carry
            scores = masked_scores(pair, key_img)
            new_max = jnp.maximum(running_max, jnp.max(scores, axis=2, keepdims=True))
            factor = jnp.exp(running_max - new_max)
            weights = jnp.exp(scores - new_max)
            new_sum = running_sum * factor + jnp.sum(weights, axis=2, keepdims=True)
            new_accum = accum * factor + weigh_values(weights, pair)
            return (new_max, new_sum, new_accum)

        return update(state)

    first_scores = masked_scores(own_pair, query_img)
    first_max = jnp.max(first_scores, axis=2, keepdims=True)
    first_weights = jnp.exp(first_scores - first_max)
    state = (
        first_max,
        jnp.sum(first_weights, axis=2, keepdims=True),
        weigh_values(first_weights, own_pair),
    )
    from_left = own_pair
    from_right = own_pair
    for step in range(1, reach + 1):
        from_left = passed_along(from_left, "blk", 1)
        state = absorb(state, from_left, token_images(me_index - step))
        from_right = passed_along(from_right, "blk", -1)
        state = absorb(state, from_right, token_images(me_index + step))
    heads_out = state[2] / state[1]
    attended = heads_out.transpose(1, 0, 2).reshape(tok, width).astype(jnp.bfloat16)
    stream = residual_in.astype(jnp.float32) + jnp.dot(
        attended, out_proj, preferred_element_type=jnp.float32
    )
    normed = layer_norm(stream, ln_gain).astype(jnp.bfloat16)
    merged = normed.reshape(row_count, 4 * width)
    feature_rows = lax.all_to_all(merged, "blk", split_axis=1, concat_axis=0, tiled=True)
    projected = lax.psum_scatter(
        jnp.dot(feature_rows, merge_proj, preferred_element_type=jnp.float32).astype(jnp.bfloat16),
        "blk",
        scatter_dimension=0,
        tiled=True,
    ).astype(jnp.float32)
    my_rows_img = row_images(me_index)
    nimg = image_rows.shape[0]
    member = (my_rows_img[:, None] == jnp.arange(nimg, dtype=jnp.int32)[None, :]).astype(
        jnp.float32
    )
    row_squares = jnp.sum(projected * projected, axis=1)
    local_sums = jnp.sum(member * row_squares[:, None], axis=0)
    spread = jnp.broadcast_to(local_sums[None, :], (blocks, local_sums.shape[0]))
    image_sums = jnp.sum(
        lax.all_to_all(spread, "blk", split_axis=0, concat_axis=0, tiled=True), axis=0
    )
    out_width = projected.shape[1]
    image_mean = image_sums / (image_rows.astype(jnp.float32) * out_width)
    row_scale = jnp.sum(member * lax.rsqrt(image_mean + 1e-06)[None, :], axis=1)
    scaled = (projected * row_scale[:, None] * out_gain[None, :]).astype(jnp.bfloat16)
    capacity = max(2, 2 * row_count // blocks)
    owner = owners[:, 0]
    onehot = (owner[:, None] == jnp.arange(blocks, dtype=jnp.int32)[None, :]).astype(jnp.int32)
    rank = jnp.sum(jnp.cumsum(onehot, axis=0) * onehot, axis=1) - 1
    slot = owner * capacity + rank
    placement = (jnp.arange(blocks * capacity, dtype=jnp.int32)[:, None] == slot[None, :]).astype(
        jnp.bfloat16
    )
    outgoing = jnp.dot(placement, scaled, preferred_element_type=jnp.float32).astype(jnp.bfloat16)
    return lax.all_to_all(outgoing, "blk", split_axis=0, concat_axis=0, tiled=True)


def solution(mesh):
    in_specs = (
        P(("dp", "blk"), None),
        P(("dp", "blk"), None),
        P(("dp", "blk"), None),
        P(("dp", "blk"), None),
        P(),
        P(),
        P("blk", None),
        P(),
        P("dp"),
        P(("dp", "blk"), None),
    )
    out_specs = P(("dp", "blk"), None)
    return jax.shard_map(
        on_device, mesh=mesh, in_specs=in_specs, out_specs=out_specs, check_vma=False
    )
```

```python
import jax
import jax.numpy as jnp
from jax import lax
from jax.sharding import PartitionSpec as P
from jax.experimental import pallas as pl
from jax.experimental.pallas import tpu as pltpu

HEADS = 16


def passed_along(value, axis, steps):
    count = lax.axis_size(axis)
    first, last = (max(0, -steps), min(count, count - steps))
    return lax.ppermute(value, axis, [(source, source + steps) for source in range(first, last)])


LANES = 128


def head_major(block, heads):
    tok, width = block.shape
    hdim = width // heads
    split = block.reshape(tok, heads, hdim).transpose(1, 0, 2)
    return jnp.pad(split, ((0, 0), (0, 0), (0, LANES - hdim)))


def attn_init(tok, heads):
    return (
        jnp.full((heads, tok, 1), -jnp.inf, jnp.float32),
        jnp.zeros((heads, tok, 1), jnp.float32),
        jnp.zeros((heads, tok, LANES), jnp.float32),
    )


def attn_finish(state, hdim):
    heads, tok, _ = state[2].shape
    out = state[2][:, :, :hdim] / state[1]
    return out.transpose(1, 0, 2).reshape(tok, heads * hdim).astype(jnp.bfloat16)


def attn_step(state, qh, kh, vh, query_img, key_img, live, scale, interpret=False):
    heads, tok, _ = qh.shape
    keys_n = kh.shape[1]

    def kernel(live_ref, q_ref, k_ref, v_ref, qi_ref, ki_ref, m_in, l_in, a_in, m_out, l_out, a_out):
        @pl.when(live_ref[0] != 0)
        def _():
            scores = lax.dot_general(
                q_ref[0], k_ref[0], (((1,), (1,)), ((), ())), preferred_element_type=jnp.float32
            ) * scale
            scores = jnp.where(qi_ref[...] == ki_ref[...], scores, -jnp.inf)
            m_prev = m_in[0]
            m_new = jnp.maximum(m_prev, jnp.max(scores, axis=1, keepdims=True))
            alpha = jnp.exp(m_prev - m_new)
            weights = jnp.exp(scores - m_new)
            l_out[0] = alpha * l_in[0] + jnp.sum(weights, axis=1, keepdims=True)
            a_out[0] = alpha * a_in[0] + jnp.dot(
                weights.astype(jnp.bfloat16), v_ref[0], preferred_element_type=jnp.float32
            )
            m_out[0] = m_new

        @pl.when(live_ref[0] == 0)
        def _():
            m_out[...] = m_in[...]
            l_out[...] = l_in[...]
            a_out[...] = a_in[...]

    head_spec = pl.BlockSpec((1, tok, LANES), lambda h, live_ref: (h, 0, 0))
    key_spec = pl.BlockSpec((1, keys_n, LANES), lambda h, live_ref: (h, 0, 0))
    stat_spec = pl.BlockSpec((1, tok, 1), lambda h, live_ref: (h, 0, 0))
    grid_spec = pltpu.PrefetchScalarGridSpec(
        num_scalar_prefetch=1,
        grid=(heads,),
        in_specs=[
            head_spec,
            key_spec,
            key_spec,
            pl.BlockSpec((tok, 1), lambda h, live_ref: (0, 0)),
            pl.BlockSpec((1, keys_n), lambda h, live_ref: (0, 0)),
            stat_spec,
            stat_spec,
            head_spec,
        ],
        out_specs=[stat_spec, stat_spec, head_spec],
    )
    return pl.pallas_call(
        kernel,
        grid_spec=grid_spec,
        out_shape=[jax.ShapeDtypeStruct(x.shape, x.dtype) for x in state],
        input_output_aliases={6: 0, 7: 1, 8: 2},
        interpret=interpret,
    )(
        live.reshape(1).astype(jnp.int32),
        qh,
        kh,
        vh,
        query_img.reshape(tok, 1),
        key_img.reshape(1, keys_n),
        *state,
    )


def layer_norm(stream, gain):
    mean = jnp.mean(stream, axis=1, keepdims=True)
    centred = stream - mean
    var = jnp.mean(centred * centred, axis=1, keepdims=True)
    return centred * lax.rsqrt(var + 1e-06) * gain[None, :]


def on_device(
    queries, keys, values, residual_in, out_proj, ln_gain, merge_proj, out_gain, image_rows, owners
):
    blocks = lax.axis_size("blk")
    me_index = lax.axis_index("blk")
    tok, width = queries.shape
    row_count = tok // 4
    heads = HEADS
    hdim = width // heads
    reach = min(6, (blocks - 1) // 2)
    scale = 1.0 / hdim**0.5
    ends = jnp.cumsum(image_rows)

    def row_images(source):
        rows = source * row_count + jnp.arange(row_count, dtype=jnp.int32)
        found = jnp.sum((rows[:, None] >= ends[None, :]).astype(jnp.int32), axis=1)
        inside = jnp.logical_and(source >= 0, source < blocks)
        return jnp.where(inside, found, -1)

    def token_images(source):
        return jnp.repeat(row_images(source), 4, total_repeat_length=tok)

    query_img = token_images(me_index)
    qh = head_major(queries, heads)
    own_pair = jnp.stack([keys, values])

    def absorb(state, pair, key_img):
        live = jnp.logical_and(
            jnp.max(key_img) >= jnp.maximum(jnp.min(query_img), 0),
            jnp.min(jnp.where(key_img >= 0, key_img, 1 << 30)) <= jnp.max(query_img),
        )
        return attn_step(
            state,
            qh,
            head_major(pair[0], heads),
            head_major(pair[1], heads),
            query_img,
            key_img,
            live,
            scale,
        )

    state = absorb(attn_init(tok, heads), own_pair, query_img)
    from_left = own_pair
    from_right = own_pair
    for step in range(1, reach + 1):
        from_left = passed_along(from_left, "blk", 1)
        state = absorb(state, from_left, token_images(me_index - step))
        from_right = passed_along(from_right, "blk", -1)
        state = absorb(state, from_right, token_images(me_index + step))
    attended = attn_finish(state, hdim)
    stream = residual_in.astype(jnp.float32) + jnp.dot(
        attended, out_proj, preferred_element_type=jnp.float32
    )
    normed = layer_norm(stream, ln_gain).astype(jnp.bfloat16)
    merged = normed.reshape(row_count, 4 * width)
    feature_rows = lax.all_to_all(merged, "blk", split_axis=1, concat_axis=0, tiled=True)
    projected = lax.psum_scatter(
        jnp.dot(feature_rows, merge_proj, preferred_element_type=jnp.float32).astype(jnp.bfloat16),
        "blk",
        scatter_dimension=0,
        tiled=True,
    ).astype(jnp.float32)
    my_rows_img = row_images(me_index)
    nimg = image_rows.shape[0]
    member = (my_rows_img[:, None] == jnp.arange(nimg, dtype=jnp.int32)[None, :]).astype(
        jnp.float32
    )
    row_squares = jnp.sum(projected * projected, axis=1)
    local_sums = jnp.sum(member * row_squares[:, None], axis=0)
    spread = jnp.broadcast_to(local_sums[None, :], (blocks, local_sums.shape[0]))
    image_sums = jnp.sum(
        lax.all_to_all(spread, "blk", split_axis=0, concat_axis=0, tiled=True), axis=0
    )
    out_width = projected.shape[1]
    image_mean = image_sums / (image_rows.astype(jnp.float32) * out_width)
    row_scale = jnp.sum(member * lax.rsqrt(image_mean + 1e-06)[None, :], axis=1)
    scaled = (projected * row_scale[:, None] * out_gain[None, :]).astype(jnp.bfloat16)
    capacity = max(2, 2 * row_count // blocks)
    owner = owners[:, 0]
    onehot = (owner[:, None] == jnp.arange(blocks, dtype=jnp.int32)[None, :]).astype(jnp.int32)
    rank = jnp.sum(jnp.cumsum(onehot, axis=0) * onehot, axis=1) - 1
    slot = owner * capacity + rank
    placement = (jnp.arange(blocks * capacity, dtype=jnp.int32)[:, None] == slot[None, :]).astype(
        jnp.bfloat16
    )
    outgoing = jnp.dot(placement, scaled, preferred_element_type=jnp.float32).astype(jnp.bfloat16)
    return lax.all_to_all(outgoing, "blk", split_axis=0, concat_axis=0, tiled=True)


def solution(mesh):
    in_specs = (
        P(("dp", "blk"), None),
        P(("dp", "blk"), None),
        P(("dp", "blk"), None),
        P(("dp", "blk"), None),
        P(),
        P(),
        P("blk", None),
        P(),
        P("dp"),
        P(("dp", "blk"), None),
    )
    out_specs = P(("dp", "blk"), None)
    return jax.shard_map(
        on_device, mesh=mesh, in_specs=in_specs, out_specs=out_specs, check_vma=False
    )
```

```python
import jax
import jax.numpy as jnp
from jax import lax
from jax.sharding import PartitionSpec as P
from jax.experimental import pallas as pl
from jax.experimental.pallas import tpu as pltpu

HEADS = 16


def passed_along(value, axis, steps):
    count = lax.axis_size(axis)
    first, last = (max(0, -steps), min(count, count - steps))
    return lax.ppermute(value, axis, [(source, source + steps) for source in range(first, last)])


LANES = 128


def head_major(block, heads):
    tok, width = block.shape
    hdim = width // heads
    split = block.reshape(tok, heads, hdim).transpose(1, 0, 2)
    return jnp.pad(split, ((0, 0), (0, 0), (0, LANES - hdim)))


def attention(qh, kh, vh, query_img, key_img, live, scale, hdim):
    heads, tok, _ = qh.shape
    n_blk = key_img.shape[0]
    blk_len = key_img.shape[2]

    def kernel(live_ref, q_ref, k_ref, v_ref, qi_ref, ki_ref, o_ref, m_sc, l_sc, a_sc):
        q = q_ref[0]
        qi = qi_ref[...]
        m_sc[...] = jnp.full(m_sc.shape, -jnp.inf, jnp.float32)
        l_sc[...] = jnp.zeros(l_sc.shape, jnp.float32)
        a_sc[...] = jnp.zeros(a_sc.shape, jnp.float32)

        def body(j, carry):
            @pl.when(live_ref[j] != 0)
            def _():
                at = pl.multiple_of(j * blk_len, blk_len)
                k = k_ref[0, pl.ds(at, blk_len), :]
                v = v_ref[0, pl.ds(at, blk_len), :]
                scores = lax.dot_general(
                    q, k, (((1,), (1,)), ((), ())), preferred_element_type=jnp.float32
                ) * scale
                scores = jnp.where(qi == ki_ref[j], scores, -jnp.inf)
                m_prev = m_sc[...]
                m_new = jnp.maximum(m_prev, jnp.max(scores, axis=1, keepdims=True))
                alpha = jnp.exp(m_prev - m_new)
                weights = jnp.exp(scores - m_new)
                l_sc[...] = alpha * l_sc[...] + jnp.sum(weights, axis=1, keepdims=True)
                a_sc[...] = alpha * a_sc[...] + jnp.dot(
                    weights.astype(jnp.bfloat16), v, preferred_element_type=jnp.float32
                )
                m_sc[...] = m_new

            return carry

        lax.fori_loop(0, n_blk, body, 0)
        o_ref[0] = a_sc[...] / l_sc[...]

    grid_spec = pltpu.PrefetchScalarGridSpec(
        num_scalar_prefetch=1,
        grid=(heads,),
        in_specs=[
            pl.BlockSpec((1, tok, LANES), lambda h, live_ref: (h, 0, 0)),
            pl.BlockSpec((1, n_blk * blk_len, LANES), lambda h, live_ref: (h, 0, 0)),
            pl.BlockSpec((1, n_blk * blk_len, LANES), lambda h, live_ref: (h, 0, 0)),
            pl.BlockSpec((tok, 1), lambda h, live_ref: (0, 0)),
            pl.BlockSpec((n_blk, 1, blk_len), lambda h, live_ref: (0, 0, 0)),
        ],
        out_specs=pl.BlockSpec((1, tok, LANES), lambda h, live_ref: (h, 0, 0)),
        scratch_shapes=[
            pltpu.VMEM((tok, 1), jnp.float32),
            pltpu.VMEM((tok, 1), jnp.float32),
            pltpu.VMEM((tok, LANES), jnp.float32),
        ],
    )
    out = pl.pallas_call(
        kernel,
        grid_spec=grid_spec,
        out_shape=jax.ShapeDtypeStruct((heads, tok, LANES), jnp.float32),
    )(live.astype(jnp.int32), qh, kh, vh, query_img.reshape(tok, 1), key_img)
    return out[:, :, :hdim].transpose(1, 0, 2).reshape(tok, heads * hdim).astype(jnp.bfloat16)

def layer_norm(stream, gain):
    mean = jnp.mean(stream, axis=1, keepdims=True)
    centred = stream - mean
    var = jnp.mean(centred * centred, axis=1, keepdims=True)
    return centred * lax.rsqrt(var + 1e-06) * gain[None, :]


def on_device(
    queries, keys, values, residual_in, out_proj, ln_gain, merge_proj, out_gain, image_rows, owners
):
    blocks = lax.axis_size("blk")
    me_index = lax.axis_index("blk")
    tok, width = queries.shape
    row_count = tok // 4
    heads = HEADS
    hdim = width // heads
    reach = min(6, (blocks - 1) // 2)
    scale = 1.0 / hdim**0.5
    ends = jnp.cumsum(image_rows)

    def row_images(source):
        rows = source * row_count + jnp.arange(row_count, dtype=jnp.int32)
        found = jnp.sum((rows[:, None] >= ends[None, :]).astype(jnp.int32), axis=1)
        inside = jnp.logical_and(source >= 0, source < blocks)
        return jnp.where(inside, found, -1)

    def token_images(source):
        return jnp.repeat(row_images(source), 4, total_repeat_length=tok)

    query_img = token_images(me_index)
    qh = head_major(queries, heads)
    own_pair = jnp.stack([keys, values])
    n_blk = 2 * reach + 1
    kh = jnp.zeros((heads, n_blk * tok, LANES), jnp.bfloat16)
    vh = jnp.zeros((heads, n_blk * tok, LANES), jnp.bfloat16)
    key_imgs = []
    lives = []

    def absorb(kh, vh, slot, pair, key_img):
        lives.append(
            jnp.logical_and(
                jnp.max(key_img) >= jnp.maximum(jnp.min(query_img), 0),
                jnp.min(jnp.where(key_img >= 0, key_img, 1 << 30)) <= jnp.max(query_img),
            )
        )
        key_imgs.append(key_img)
        kh = kh.at[:, slot * tok : (slot + 1) * tok, :].set(head_major(pair[0], heads))
        vh = vh.at[:, slot * tok : (slot + 1) * tok, :].set(head_major(pair[1], heads))
        return kh, vh

    kh, vh = absorb(kh, vh, 0, own_pair, query_img)
    from_left = own_pair
    from_right = own_pair
    for step in range(1, reach + 1):
        from_left = passed_along(from_left, "blk", 1)
        kh, vh = absorb(kh, vh, 2 * step - 1, from_left, token_images(me_index - step))
        from_right = passed_along(from_right, "blk", -1)
        kh, vh = absorb(kh, vh, 2 * step, from_right, token_images(me_index + step))
    attended = attention(
        qh,
        kh,
        vh,
        query_img,
        jnp.stack(key_imgs).reshape(n_blk, 1, tok),
        jnp.stack(lives),
        scale,
        hdim,
    )
    stream = residual_in.astype(jnp.float32) + jnp.dot(
        attended, out_proj, preferred_element_type=jnp.float32
    )
    normed = layer_norm(stream, ln_gain).astype(jnp.bfloat16)
    merged = normed.reshape(row_count, 4 * width)
    feature_rows = lax.all_to_all(merged, "blk", split_axis=1, concat_axis=0, tiled=True)
    projected = lax.psum_scatter(
        jnp.dot(feature_rows, merge_proj, preferred_element_type=jnp.float32).astype(jnp.bfloat16),
        "blk",
        scatter_dimension=0,
        tiled=True,
    ).astype(jnp.float32)
    my_rows_img = row_images(me_index)
    nimg = image_rows.shape[0]
    member = (my_rows_img[:, None] == jnp.arange(nimg, dtype=jnp.int32)[None, :]).astype(
        jnp.float32
    )
    row_squares = jnp.sum(projected * projected, axis=1)
    local_sums = jnp.sum(member * row_squares[:, None], axis=0)
    spread = jnp.broadcast_to(local_sums[None, :], (blocks, local_sums.shape[0]))
    image_sums = jnp.sum(
        lax.all_to_all(spread, "blk", split_axis=0, concat_axis=0, tiled=True), axis=0
    )
    out_width = projected.shape[1]
    image_mean = image_sums / (image_rows.astype(jnp.float32) * out_width)
    row_scale = jnp.sum(member * lax.rsqrt(image_mean + 1e-06)[None, :], axis=1)
    scaled = (projected * row_scale[:, None] * out_gain[None, :]).astype(jnp.bfloat16)
    capacity = max(2, 2 * row_count // blocks)
    owner = owners[:, 0]
    onehot = (owner[:, None] == jnp.arange(blocks, dtype=jnp.int32)[None, :]).astype(jnp.int32)
    rank = jnp.sum(jnp.cumsum(onehot, axis=0) * onehot, axis=1) - 1
    slot = owner * capacity + rank
    placement = (jnp.arange(blocks * capacity, dtype=jnp.int32)[:, None] == slot[None, :]).astype(
        jnp.bfloat16
    )
    outgoing = jnp.dot(placement, scaled, preferred_element_type=jnp.float32).astype(jnp.bfloat16)
    return lax.all_to_all(outgoing, "blk", split_axis=0, concat_axis=0, tiled=True)


def solution(mesh):
    in_specs = (
        P(("dp", "blk"), None),
        P(("dp", "blk"), None),
        P(("dp", "blk"), None),
        P(("dp", "blk"), None),
        P(),
        P(),
        P("blk", None),
        P(),
        P("dp"),
        P(("dp", "blk"), None),
    )
    out_specs = P(("dp", "blk"), None)
    return jax.shard_map(
        on_device, mesh=mesh, in_specs=in_specs, out_specs=out_specs, check_vma=False
    )
```

```python
import jax
import jax.numpy as jnp
from jax import lax
from jax.sharding import PartitionSpec as P
from jax.experimental import pallas as pl
from jax.experimental.pallas import tpu as pltpu

HEADS = 16


def passed_along(value, axis, steps):
    count = lax.axis_size(axis)
    first, last = (max(0, -steps), min(count, count - steps))
    return lax.ppermute(value, axis, [(source, source + steps) for source in range(first, last)])


LANES = 128


def attention(queries, pairs, query_img, key_img, live, scale, heads):
    tok, width = queries.shape
    hdim = width // heads
    n_blk = pairs.shape[0]

    def kernel(live_ref, q_ref, kv_ref, qi_ref, ki_ref, o_ref, m_sc, l_sc, a_sc):
        j = pl.program_id(0)

        @pl.when(j == 0)
        def _():
            m_sc[...] = jnp.full(m_sc.shape, -jnp.inf, jnp.float32)
            l_sc[...] = jnp.zeros(l_sc.shape, jnp.float32)
            a_sc[...] = jnp.zeros(a_sc.shape, jnp.float32)

        @pl.when(live_ref[j] != 0)
        def _():
            same = qi_ref[...] == ki_ref[0]
            for h in range(heads):
                cols = slice(h * hdim, (h + 1) * hdim)
                q = q_ref[:, cols]
                k = kv_ref[0, 0, :, cols]
                v = kv_ref[0, 1, :, cols]
                scores = lax.dot_general(
                    q, k, (((1,), (1,)), ((), ())), preferred_element_type=jnp.float32
                ) * scale
                scores = jnp.where(same, scores, -jnp.inf)
                m_prev = m_sc[h]
                m_new = jnp.maximum(m_prev, jnp.max(scores, axis=1, keepdims=True))
                alpha = jnp.exp(m_prev - m_new)
                weights = jnp.exp(scores - m_new)
                l_sc[h] = alpha * l_sc[h] + jnp.sum(weights, axis=1, keepdims=True)
                a_sc[h] = alpha * a_sc[h] + jnp.dot(
                    weights.astype(jnp.bfloat16), v, preferred_element_type=jnp.float32
                )
                m_sc[h] = m_new

        @pl.when(j == n_blk - 1)
        def _():
            o_ref[...] = a_sc[...] / l_sc[...]

    grid_spec = pltpu.PrefetchScalarGridSpec(
        num_scalar_prefetch=1,
        grid=(n_blk,),
        in_specs=[
            pl.BlockSpec((tok, width), lambda j, live_ref: (0, 0)),
            pl.BlockSpec(
                (1, 2, tok, width), lambda j, live_ref: (j * live_ref[j], 0, 0, 0)
            ),
            pl.BlockSpec((tok, 1), lambda j, live_ref: (0, 0)),
            pl.BlockSpec((1, 1, tok), lambda j, live_ref: (j, 0, 0)),
        ],
        out_specs=pl.BlockSpec((heads, tok, hdim), lambda j, live_ref: (0, 0, 0)),
        scratch_shapes=[
            pltpu.VMEM((heads, tok, 1), jnp.float32),
            pltpu.VMEM((heads, tok, 1), jnp.float32),
            pltpu.VMEM((heads, tok, hdim), jnp.float32),
        ],
    )
    out = pl.pallas_call(
        kernel,
        grid_spec=grid_spec,
        out_shape=jax.ShapeDtypeStruct((heads, tok, hdim), jnp.float32),
    )(live.astype(jnp.int32), queries, pairs, query_img.reshape(tok, 1), key_img)
    return out.transpose(1, 0, 2).reshape(tok, width).astype(jnp.bfloat16)

def layer_norm(stream, gain):
    mean = jnp.mean(stream, axis=1, keepdims=True)
    centred = stream - mean
    var = jnp.mean(centred * centred, axis=1, keepdims=True)
    return centred * lax.rsqrt(var + 1e-06) * gain[None, :]


def on_device(
    queries, keys, values, residual_in, out_proj, ln_gain, merge_proj, out_gain, image_rows, owners
):
    blocks = lax.axis_size("blk")
    me_index = lax.axis_index("blk")
    tok, width = queries.shape
    row_count = tok // 4
    heads = HEADS
    hdim = width // heads
    reach = min(6, (blocks - 1) // 2)
    scale = 1.0 / hdim**0.5
    ends = jnp.cumsum(image_rows)

    def row_images(source):
        rows = source * row_count + jnp.arange(row_count, dtype=jnp.int32)
        found = jnp.sum((rows[:, None] >= ends[None, :]).astype(jnp.int32), axis=1)
        inside = jnp.logical_and(source >= 0, source < blocks)
        return jnp.where(inside, found, -1)

    def token_images(source):
        return jnp.repeat(row_images(source), 4, total_repeat_length=tok)

    query_img = token_images(me_index)
    own_pair = jnp.stack([keys, values])
    n_blk = 2 * reach + 1
    pairs = jnp.zeros((n_blk,) + own_pair.shape, own_pair.dtype)
    key_imgs = []
    lives = []

    def absorb(pairs, slot, pair, key_img):
        lives.append(
            jnp.logical_and(
                jnp.max(key_img) >= jnp.maximum(jnp.min(query_img), 0),
                jnp.min(jnp.where(key_img >= 0, key_img, 1 << 30)) <= jnp.max(query_img),
            )
        )
        key_imgs.append(key_img)
        return lax.dynamic_update_slice(pairs, pair[None], (slot, 0, 0, 0))

    pairs = absorb(pairs, 0, own_pair, query_img)
    from_left = own_pair
    from_right = own_pair
    for step in range(1, reach + 1):
        from_left = passed_along(from_left, "blk", 1)
        pairs = absorb(pairs, 2 * step - 1, from_left, token_images(me_index - step))
        from_right = passed_along(from_right, "blk", -1)
        pairs = absorb(pairs, 2 * step, from_right, token_images(me_index + step))
    attended = attention(
        queries,
        pairs,
        query_img,
        jnp.stack(key_imgs).reshape(n_blk, 1, tok),
        jnp.stack(lives),
        scale,
        heads,
    )
    stream = residual_in.astype(jnp.float32) + jnp.dot(
        attended, out_proj, preferred_element_type=jnp.float32
    )
    normed = layer_norm(stream, ln_gain).astype(jnp.bfloat16)
    merged = normed.reshape(row_count, 4 * width)
    feature_rows = lax.all_to_all(merged, "blk", split_axis=1, concat_axis=0, tiled=True)
    projected = lax.psum_scatter(
        jnp.dot(feature_rows, merge_proj, preferred_element_type=jnp.float32).astype(jnp.bfloat16),
        "blk",
        scatter_dimension=0,
        tiled=True,
    ).astype(jnp.float32)
    my_rows_img = row_images(me_index)
    nimg = image_rows.shape[0]
    member = (my_rows_img[:, None] == jnp.arange(nimg, dtype=jnp.int32)[None, :]).astype(
        jnp.float32
    )
    row_squares = jnp.sum(projected * projected, axis=1)
    local_sums = jnp.sum(member * row_squares[:, None], axis=0)
    spread = jnp.broadcast_to(local_sums[None, :], (blocks, local_sums.shape[0]))
    image_sums = jnp.sum(
        lax.all_to_all(spread, "blk", split_axis=0, concat_axis=0, tiled=True), axis=0
    )
    out_width = projected.shape[1]
    image_mean = image_sums / (image_rows.astype(jnp.float32) * out_width)
    row_scale = jnp.sum(member * lax.rsqrt(image_mean + 1e-06)[None, :], axis=1)
    scaled = (projected * row_scale[:, None] * out_gain[None, :]).astype(jnp.bfloat16)
    capacity = max(2, 2 * row_count // blocks)
    owner = owners[:, 0]
    onehot = (owner[:, None] == jnp.arange(blocks, dtype=jnp.int32)[None, :]).astype(jnp.int32)
    rank = jnp.sum(jnp.cumsum(onehot, axis=0) * onehot, axis=1) - 1
    slot = owner * capacity + rank
    placement = (jnp.arange(blocks * capacity, dtype=jnp.int32)[:, None] == slot[None, :]).astype(
        jnp.bfloat16
    )
    outgoing = jnp.dot(placement, scaled, preferred_element_type=jnp.float32).astype(jnp.bfloat16)
    return lax.all_to_all(outgoing, "blk", split_axis=0, concat_axis=0, tiled=True)


def solution(mesh):
    in_specs = (
        P(("dp", "blk"), None),
        P(("dp", "blk"), None),
        P(("dp", "blk"), None),
        P(("dp", "blk"), None),
        P(),
        P(),
        P("blk", None),
        P(),
        P("dp"),
        P(("dp", "blk"), None),
    )
    out_specs = P(("dp", "blk"), None)
    return jax.shard_map(
        on_device, mesh=mesh, in_specs=in_specs, out_specs=out_specs, check_vma=False
    )
```

```python
import jax
import jax.numpy as jnp
from jax import lax
from jax.sharding import PartitionSpec as P

HEADS = 16


def passed_along(value, axis, steps):
    count = lax.axis_size(axis)
    first, last = (max(0, -steps), min(count, count - steps))
    return lax.ppermute(value, axis, [(source, source + steps) for source in range(first, last)])


def layer_norm(stream, gain):
    mean = jnp.mean(stream, axis=1, keepdims=True)
    centred = stream - mean
    var = jnp.mean(centred * centred, axis=1, keepdims=True)
    return centred * lax.rsqrt(var + 1e-06) * gain[None, :]


def on_device(
    queries, keys, values, residual_in, out_proj, ln_gain, merge_proj, out_gain, image_rows, owners
):
    blocks = lax.axis_size("blk")
    me_index = lax.axis_index("blk")
    tok, width = queries.shape
    row_count = tok // 4
    heads = HEADS
    hdim = width // heads
    reach = min(6, (blocks - 1) // 2)
    scale = 1.0 / hdim**0.5
    ends = jnp.cumsum(image_rows)

    def row_images(source):
        rows = source * row_count + jnp.arange(row_count, dtype=jnp.int32)
        found = jnp.sum((rows[:, None] >= ends[None, :]).astype(jnp.int32), axis=1)
        inside = jnp.logical_and(source >= 0, source < blocks)
        return jnp.where(inside, found, -1)

    def token_images(source):
        return jnp.repeat(row_images(source), 4, total_repeat_length=tok)

    query_img = token_images(me_index)
    q_heads = queries.reshape(tok, heads, hdim)
    own_pair = jnp.stack([keys, values])

    def masked_scores(pair, key_img):
        k_heads = pair[0].reshape(-1, heads, hdim)
        scores = (
            jnp.einsum("qhd,khd->hqk", q_heads, k_heads, preferred_element_type=jnp.float32) * scale
        )
        return jnp.where(query_img[None, :, None] == key_img[None, None, :], scores, -jnp.inf)

    def weigh_values(weights, pair):
        v_heads = pair[1].reshape(-1, heads, hdim)
        return jnp.einsum(
            "hqk,khd->hqd",
            weights.astype(jnp.bfloat16),
            v_heads,
            preferred_element_type=jnp.float32,
        )

    def absorb(state, pair, key_img):

        def update(carry):
            running_max, running_sum, accum = carry
            scores = masked_scores(pair, key_img)
            new_max = jnp.maximum(running_max, jnp.max(scores, axis=2, keepdims=True))
            factor = jnp.exp(running_max - new_max)
            weights = jnp.exp(scores - new_max)
            new_sum = running_sum * factor + jnp.sum(weights, axis=2, keepdims=True)
            new_accum = accum * factor + weigh_values(weights, pair)
            return (new_max, new_sum, new_accum)

        live = jnp.logical_and(
            jnp.max(key_img) >= jnp.maximum(jnp.min(query_img), 0),
            jnp.min(jnp.where(key_img >= 0, key_img, 1 << 30)) <= jnp.max(query_img),
        )
        return lax.cond(live, update, lambda carry: carry, state)

    first_scores = masked_scores(own_pair, query_img)
    first_max = jnp.max(first_scores, axis=2, keepdims=True)
    first_weights = jnp.exp(first_scores - first_max)
    state = (
        first_max,
        jnp.sum(first_weights, axis=2, keepdims=True),
        weigh_values(first_weights, own_pair),
    )
    from_left = own_pair
    from_right = own_pair
    for step in range(1, reach + 1):
        from_left = passed_along(from_left, "blk", 1)
        state = absorb(state, from_left, token_images(me_index - step))
        from_right = passed_along(from_right, "blk", -1)
        state = absorb(state, from_right, token_images(me_index + step))
    heads_out = state[2] / state[1]
    attended = heads_out.transpose(1, 0, 2).reshape(tok, width).astype(jnp.bfloat16)
    stream = residual_in.astype(jnp.float32) + jnp.dot(
        attended, out_proj, preferred_element_type=jnp.float32
    )
    normed = layer_norm(stream, ln_gain).astype(jnp.bfloat16)
    merged = normed.reshape(row_count, 4 * width)
    feature_rows = lax.all_to_all(merged, "blk", split_axis=1, concat_axis=0, tiled=True)
    projected = lax.psum_scatter(
        jnp.dot(feature_rows, merge_proj, preferred_element_type=jnp.float32).astype(jnp.bfloat16),
        "blk",
        scatter_dimension=0,
        tiled=True,
    ).astype(jnp.float32)
    my_rows_img = row_images(me_index)
    nimg = image_rows.shape[0]
    member = (my_rows_img[:, None] == jnp.arange(nimg, dtype=jnp.int32)[None, :]).astype(
        jnp.float32
    )
    row_squares = jnp.sum(projected * projected, axis=1)
    local_sums = jnp.sum(member * row_squares[:, None], axis=0)
    spread = jnp.broadcast_to(local_sums[None, :], (blocks, local_sums.shape[0]))
    image_sums = jnp.sum(
        lax.all_to_all(spread, "blk", split_axis=0, concat_axis=0, tiled=True), axis=0
    )
    out_width = projected.shape[1]
    image_mean = image_sums / (image_rows.astype(jnp.float32) * out_width)
    row_scale = jnp.sum(member * lax.rsqrt(image_mean + 1e-06)[None, :], axis=1)
    scaled = (projected * row_scale[:, None] * out_gain[None, :]).astype(jnp.bfloat16)
    capacity = max(2, 2 * row_count // blocks)
    owner = owners[:, 0]
    onehot = (owner[:, None] == jnp.arange(blocks, dtype=jnp.int32)[None, :]).astype(jnp.int32)
    rank = jnp.sum(jnp.cumsum(onehot, axis=0) * onehot, axis=1) - 1
    slot = owner * capacity + rank
    placement = (jnp.arange(blocks * capacity, dtype=jnp.int32)[:, None] == slot[None, :]).astype(
        jnp.bfloat16
    )
    outgoing = jnp.dot(placement, scaled, preferred_element_type=jnp.float32).astype(jnp.bfloat16)
    return lax.all_to_all(outgoing, "blk", split_axis=0, concat_axis=0, tiled=True)


def solution(mesh):
    in_specs = (
        P(("dp", "blk"), None),
        P(("dp", "blk"), None),
        P(("dp", "blk"), None),
        P(("dp", "blk"), None),
        P(),
        P(),
        P("blk", None),
        P(),
        P("dp"),
        P(("dp", "blk"), None),
    )
    out_specs = P(("dp", "blk"), None)
    return jax.shard_map(
        on_device, mesh=mesh, in_specs=in_specs, out_specs=out_specs, check_vma=False
    )
```

```python
import jax
import jax.numpy as jnp
from jax import lax
from jax.sharding import PartitionSpec as P

HEADS = 16


BLK = ("chip", "core")


def passed_along(value, axis, steps):
    count = lax.axis_size("chip") * lax.axis_size("core")
    first, last = (max(0, -steps), min(count, count - steps))
    return lax.ppermute(value, axis, [(source, source + steps) for source in range(first, last)])


def layer_norm(stream, gain):
    mean = jnp.mean(stream, axis=1, keepdims=True)
    centred = stream - mean
    var = jnp.mean(centred * centred, axis=1, keepdims=True)
    return centred * lax.rsqrt(var + 1e-06) * gain[None, :]


def on_device(
    queries, keys, values, residual_in, out_proj, ln_gain, merge_proj, out_gain, image_rows, owners
):
    chips = lax.axis_size("chip")
    cores = lax.axis_size("core")
    blocks = chips * cores
    me_index = lax.axis_index("chip") * cores + lax.axis_index("core")
    tok, width = queries.shape
    row_count = tok // 4
    heads = HEADS
    hdim = width // heads
    reach = min(6, (blocks - 1) // 2)
    scale = 1.0 / hdim**0.5
    ends = jnp.cumsum(image_rows)

    def row_images(source):
        rows = source * row_count + jnp.arange(row_count, dtype=jnp.int32)
        found = jnp.sum((rows[:, None] >= ends[None, :]).astype(jnp.int32), axis=1)
        inside = jnp.logical_and(source >= 0, source < blocks)
        return jnp.where(inside, found, -1)

    def token_images(source):
        return jnp.repeat(row_images(source), 4, total_repeat_length=tok)

    query_img = token_images(me_index)
    q_heads = queries.reshape(tok, heads, hdim)
    own_pair = jnp.stack([keys, values])

    def masked_scores(pair, key_img):
        k_heads = pair[0].reshape(-1, heads, hdim)
        scores = (
            jnp.einsum("qhd,khd->hqk", q_heads, k_heads, preferred_element_type=jnp.float32) * scale
        )
        return jnp.where(query_img[None, :, None] == key_img[None, None, :], scores, -jnp.inf)

    def weigh_values(weights, pair):
        v_heads = pair[1].reshape(-1, heads, hdim)
        return jnp.einsum(
            "hqk,khd->hqd",
            weights.astype(jnp.bfloat16),
            v_heads,
            preferred_element_type=jnp.float32,
        )

    def absorb(state, pair, key_img):

        def update(carry):
            running_max, running_sum, accum = carry
            scores = masked_scores(pair, key_img)
            new_max = jnp.maximum(running_max, jnp.max(scores, axis=2, keepdims=True))
            factor = jnp.exp(running_max - new_max)
            weights = jnp.exp(scores - new_max)
            new_sum = running_sum * factor + jnp.sum(weights, axis=2, keepdims=True)
            new_accum = accum * factor + weigh_values(weights, pair)
            return (new_max, new_sum, new_accum)

        live = jnp.logical_and(
            jnp.max(key_img) >= jnp.maximum(jnp.min(query_img), 0),
            jnp.min(jnp.where(key_img >= 0, key_img, 1 << 30)) <= jnp.max(query_img),
        )
        return lax.cond(live, update, lambda carry: carry, state)

    first_scores = masked_scores(own_pair, query_img)
    first_max = jnp.max(first_scores, axis=2, keepdims=True)
    first_weights = jnp.exp(first_scores - first_max)
    state = (
        first_max,
        jnp.sum(first_weights, axis=2, keepdims=True),
        weigh_values(first_weights, own_pair),
    )
    from_left = own_pair
    from_right = own_pair
    for step in range(1, reach + 1):
        from_left = passed_along(from_left, BLK, 1)
        state = absorb(state, from_left, token_images(me_index - step))
        from_right = passed_along(from_right, BLK, -1)
        state = absorb(state, from_right, token_images(me_index + step))
    heads_out = state[2] / state[1]
    attended = heads_out.transpose(1, 0, 2).reshape(tok, width).astype(jnp.bfloat16)
    stream = residual_in.astype(jnp.float32) + jnp.dot(
        attended, out_proj, preferred_element_type=jnp.float32
    )
    normed = layer_norm(stream, ln_gain).astype(jnp.bfloat16)
    merged = normed.reshape(row_count, 4 * width)
    feat = merge_proj.shape[0]
    out_width = merge_proj.shape[1]
    half = out_width // cores
    core_index = lax.axis_index("core")
    chip_index = lax.axis_index("chip")
    chip_weights = lax.all_to_all(merge_proj, "core", split_axis=1, concat_axis=0, tiled=True)
    by_chip = lax.all_to_all(
        merged.reshape(row_count, chips, cores * feat), "chip", split_axis=1, concat_axis=0, tiled=True
    )
    chip_rows = lax.all_gather(
        by_chip.reshape(chips, 1, row_count, cores * feat), "core", axis=1, tiled=True
    ).reshape(
        chips * cores * row_count, cores * feat
    )
    partial = jnp.dot(chip_rows, chip_weights, preferred_element_type=jnp.float32).astype(jnp.bfloat16)
    projected = lax.psum_scatter(partial, "chip", scatter_dimension=0, tiled=True).astype(jnp.float32)
    pair_rows = cores * row_count
    rows = chip_index * pair_rows + jnp.arange(pair_rows, dtype=jnp.int32)
    my_rows_img = jnp.sum((rows[:, None] >= ends[None, :]).astype(jnp.int32), axis=1)
    nimg = image_rows.shape[0]
    member = (my_rows_img[:, None] == jnp.arange(nimg, dtype=jnp.int32)[None, :]).astype(
        jnp.float32
    )
    row_squares = jnp.sum(projected * projected, axis=1)
    local_sums = jnp.sum(member * row_squares[:, None], axis=0)
    spread = jnp.broadcast_to(local_sums[None, :], (blocks, nimg))
    image_sums = jnp.sum(lax.all_to_all(spread, BLK, split_axis=0, concat_axis=0, tiled=True), axis=0)
    image_mean = image_sums / (image_rows.astype(jnp.float32) * out_width)
    row_scale = jnp.sum(member * lax.rsqrt(image_mean + 1e-06)[None, :], axis=1)
    my_gain = lax.dynamic_slice_in_dim(out_gain, core_index * half, half)
    scaled = (projected * row_scale[:, None] * my_gain[None, :]).astype(jnp.bfloat16)
    capacity = max(2, 2 * row_count // blocks)
    owner = lax.all_to_all(
        jnp.broadcast_to(owners[:, 0][None, :], (cores, row_count)),
        "core",
        split_axis=0,
        concat_axis=0,
        tiled=True,
    )
    onehot = (owner[:, :, None] == jnp.arange(blocks, dtype=jnp.int32)[None, None, :]).astype(jnp.int32)
    rank = jnp.sum(jnp.cumsum(onehot, axis=1) * onehot, axis=2) - 1
    slot = (
        owner * (cores * capacity)
        + jnp.arange(cores, dtype=jnp.int32)[:, None] * capacity
        + rank
    ).reshape(pair_rows)
    placement = (
        jnp.arange(blocks * cores * capacity, dtype=jnp.int32)[:, None] == slot[None, :]
    ).astype(jnp.bfloat16)
    outgoing = jnp.dot(placement, scaled, preferred_element_type=jnp.float32).astype(jnp.bfloat16)
    incoming = lax.all_to_all(outgoing, BLK, split_axis=0, concat_axis=0, tiled=True)
    return (
        incoming.reshape(chips, cores, cores, capacity, half)
        .transpose(0, 2, 3, 1, 4)
        .reshape(blocks * capacity, out_width)
    )


def solution(mesh):
    devices = mesh.devices
    cores = 2
    split_mesh = jax.sharding.Mesh(
        devices.reshape(devices.shape[0], devices.shape[1] // cores, cores), ("dp", "chip", "core")
    )
    rows = P(("dp", "chip", "core"), None)
    in_specs = (rows, rows, rows, rows, P(), P(), P(("chip", "core"), None), P(), P("dp"), rows)
    return jax.shard_map(
        on_device, mesh=split_mesh, in_specs=in_specs, out_specs=rows, check_vma=False
    )
```

```python
import jax
import jax.numpy as jnp
from jax import lax
from jax.sharding import PartitionSpec as P

HEADS = 16


BLK = ("chip", "core")


def passed_along(value, axis, steps):
    count = lax.axis_size("chip") * lax.axis_size("core")
    first, last = (max(0, -steps), min(count, count - steps))
    return lax.ppermute(value, axis, [(source, source + steps) for source in range(first, last)])


def layer_norm(stream, gain):
    mean = jnp.mean(stream, axis=1, keepdims=True)
    centred = stream - mean
    var = jnp.mean(centred * centred, axis=1, keepdims=True)
    return centred * lax.rsqrt(var + 1e-06) * gain[None, :]


def on_device(
    queries, keys, values, residual_in, out_proj, ln_gain, merge_proj, out_gain, image_rows, owners
):
    chips = lax.axis_size("chip")
    cores = lax.axis_size("core")
    blocks = chips * cores
    me_index = lax.axis_index("chip") * cores + lax.axis_index("core")
    tok, width = queries.shape
    row_count = tok // 4
    heads = HEADS
    hdim = width // heads
    reach = min(6, (blocks - 1) // 2)
    scale = 1.0 / hdim**0.5
    ends = jnp.cumsum(image_rows)

    def row_images(source):
        rows = source * row_count + jnp.arange(row_count, dtype=jnp.int32)
        found = jnp.sum((rows[:, None] >= ends[None, :]).astype(jnp.int32), axis=1)
        inside = jnp.logical_and(source >= 0, source < blocks)
        return jnp.where(inside, found, -1)

    def token_images(source):
        rows = source * row_count + jnp.arange(tok, dtype=jnp.int32) // 4
        found = jnp.sum((rows[:, None] >= ends[None, :]).astype(jnp.int32), axis=1)
        inside = jnp.logical_and(source >= 0, source < blocks)
        return jnp.where(inside, found, -1)

    query_img = token_images(me_index)
    q_heads = queries.reshape(tok, heads, hdim)
    own_pair = jnp.stack([keys, values])

    def masked_scores(pair, key_img):
        k_heads = pair[0].reshape(-1, heads, hdim)
        scores = (
            jnp.einsum("qhd,khd->hqk", q_heads, k_heads, preferred_element_type=jnp.float32) * scale
        )
        return jnp.where(query_img[None, :, None] == key_img[None, None, :], scores, -jnp.inf)

    def weigh_values(weights, pair):
        v_heads = pair[1].reshape(-1, heads, hdim)
        return jnp.einsum(
            "hqk,khd->hqd",
            weights.astype(jnp.bfloat16),
            v_heads,
            preferred_element_type=jnp.float32,
        )

    def absorb(state, pair, key_img):

        def update(carry):
            running_max, running_sum, accum = carry
            scores = masked_scores(pair, key_img)
            new_max = jnp.maximum(running_max, jnp.max(scores, axis=2, keepdims=True))
            factor = jnp.exp(running_max - new_max)
            weights = jnp.exp(scores - new_max)
            new_sum = running_sum * factor + jnp.sum(weights, axis=2, keepdims=True)
            new_accum = accum * factor + weigh_values(weights, pair)
            return (new_max, new_sum, new_accum)

        live = jnp.logical_and(
            jnp.max(key_img) >= jnp.maximum(jnp.min(query_img), 0),
            jnp.min(jnp.where(key_img >= 0, key_img, 1 << 30)) <= jnp.max(query_img),
        )
        return lax.cond(live, update, lambda carry: carry, state)

    first_scores = masked_scores(own_pair, query_img)
    first_max = jnp.max(first_scores, axis=2, keepdims=True)
    first_weights = jnp.exp(first_scores - first_max)
    state = (
        first_max,
        jnp.sum(first_weights, axis=2, keepdims=True),
        weigh_values(first_weights, own_pair),
    )
    from_left = own_pair
    from_right = own_pair
    for step in range(1, reach + 1):
        from_left = passed_along(from_left, BLK, 1)
        state = absorb(state, from_left, token_images(me_index - step))
        from_right = passed_along(from_right, BLK, -1)
        state = absorb(state, from_right, token_images(me_index + step))
    heads_out = state[2] / state[1]
    attended = heads_out.transpose(1, 0, 2).reshape(tok, width).astype(jnp.bfloat16)
    stream = residual_in.astype(jnp.float32) + jnp.dot(
        attended, out_proj, preferred_element_type=jnp.float32
    )
    normed = layer_norm(stream, ln_gain).astype(jnp.bfloat16)
    merged = normed.reshape(row_count, 4 * width)
    feat = merge_proj.shape[0]
    out_width = merge_proj.shape[1]
    half = out_width // cores
    core_index = lax.axis_index("core")
    chip_index = lax.axis_index("chip")
    chip_weights = lax.all_to_all(merge_proj, "core", split_axis=1, concat_axis=0, tiled=True)
    by_chip = lax.all_to_all(
        merged.reshape(row_count, chips, cores * feat), "chip", split_axis=1, concat_axis=0, tiled=True
    )
    chip_rows = lax.all_gather(
        by_chip.reshape(chips, 1, row_count, cores * feat), "core", axis=1, tiled=True
    ).reshape(
        chips * cores * row_count, cores * feat
    )
    partial = jnp.dot(chip_rows, chip_weights, preferred_element_type=jnp.float32).astype(jnp.bfloat16)
    projected = lax.psum_scatter(partial, "chip", scatter_dimension=0, tiled=True).astype(jnp.float32)
    pair_rows = cores * row_count
    rows = chip_index * pair_rows + jnp.arange(pair_rows, dtype=jnp.int32)
    my_rows_img = jnp.sum((rows[:, None] >= ends[None, :]).astype(jnp.int32), axis=1)
    nimg = image_rows.shape[0]
    member = (my_rows_img[:, None] == jnp.arange(nimg, dtype=jnp.int32)[None, :]).astype(
        jnp.float32
    )
    row_squares = jnp.sum(projected * projected, axis=1)
    local_sums = jnp.sum(member * row_squares[:, None], axis=0)
    spread = jnp.broadcast_to(local_sums[None, :], (blocks, nimg))
    image_sums = jnp.sum(lax.all_to_all(spread, BLK, split_axis=0, concat_axis=0, tiled=True), axis=0)
    image_mean = image_sums / (image_rows.astype(jnp.float32) * out_width)
    row_scale = jnp.sum(member * lax.rsqrt(image_mean + 1e-06)[None, :], axis=1)
    my_gain = lax.dynamic_slice_in_dim(out_gain, core_index * half, half)
    scaled = (projected * row_scale[:, None] * my_gain[None, :]).astype(jnp.bfloat16)
    capacity = max(2, 2 * row_count // blocks)
    owner = lax.all_to_all(
        jnp.broadcast_to(owners[:, 0][None, :], (cores, row_count)),
        "core",
        split_axis=0,
        concat_axis=0,
        tiled=True,
    )
    onehot = (owner[:, :, None] == jnp.arange(blocks, dtype=jnp.int32)[None, None, :]).astype(jnp.int32)
    rank = jnp.sum(jnp.cumsum(onehot, axis=1) * onehot, axis=2) - 1
    slot = (
        owner * (cores * capacity)
        + jnp.arange(cores, dtype=jnp.int32)[:, None] * capacity
        + rank
    ).reshape(pair_rows)
    placement = (
        jnp.arange(blocks * cores * capacity, dtype=jnp.int32)[:, None] == slot[None, :]
    ).astype(jnp.bfloat16)
    outgoing = jnp.dot(placement, scaled, preferred_element_type=jnp.float32).astype(jnp.bfloat16)
    incoming = lax.all_to_all(outgoing, BLK, split_axis=0, concat_axis=0, tiled=True)
    return (
        incoming.reshape(chips, cores, cores, capacity, half)
        .transpose(0, 2, 3, 1, 4)
        .reshape(blocks * capacity, out_width)
    )


def solution(mesh):
    devices = mesh.devices
    cores = 2
    split_mesh = jax.sharding.Mesh(
        devices.reshape(devices.shape[0], devices.shape[1] // cores, cores), ("dp", "chip", "core")
    )
    rows = P(("dp", "chip", "core"), None)
    in_specs = (rows, rows, rows, rows, P(), P(), P(("chip", "core"), None), P(), P("dp"), rows)
    return jax.shard_map(
        on_device, mesh=split_mesh, in_specs=in_specs, out_specs=rows, check_vma=False
    )
```

```python
import jax
import jax.numpy as jnp
from jax import lax
from jax.sharding import PartitionSpec as P

HEADS = 16


BLK = ("chip", "core")


def passed_along(value, axis, steps):
    count = lax.axis_size("chip") * lax.axis_size("core")
    first, last = (max(0, -steps), min(count, count - steps))
    return lax.ppermute(value, axis, [(source, source + steps) for source in range(first, last)])


def layer_norm(stream, gain):
    mean = jnp.mean(stream, axis=1, keepdims=True)
    centred = stream - mean
    var = jnp.mean(centred * centred, axis=1, keepdims=True)
    return centred * lax.rsqrt(var + 1e-06) * gain[None, :]


def on_device(
    queries, keys, values, residual_in, out_proj, ln_gain, merge_proj, out_gain, image_rows, owners
):
    chips = lax.axis_size("chip")
    cores = lax.axis_size("core")
    blocks = chips * cores
    me_index = lax.axis_index("chip") * cores + lax.axis_index("core")
    tok, width = queries.shape
    row_count = tok // 4
    heads = HEADS
    hdim = width // heads
    reach = min(6, (blocks - 1) // 2)
    scale = 1.0 / hdim**0.5
    ends = jnp.cumsum(image_rows)

    def token_images(source):
        rows = source * row_count + jnp.arange(tok, dtype=jnp.int32) // 4
        found = jnp.sum((rows[:, None] >= ends[None, :]).astype(jnp.int32), axis=1)
        inside = jnp.logical_and(source >= 0, source < blocks)
        return jnp.where(inside, found, -1)

    query_img = token_images(me_index)
    q_heads = queries.reshape(tok, heads, hdim)
    own_pair = jnp.stack([keys, values])

    def masked_scores(pair, key_img):
        k_heads = pair[0].reshape(-1, heads, hdim)
        scores = (
            jnp.einsum("qhd,khd->hqk", q_heads, k_heads, preferred_element_type=jnp.float32) * scale
        )
        return jnp.where(query_img[None, :, None] == key_img[None, None, :], scores, -jnp.inf)

    def weigh_values(weights, pair):
        v_heads = pair[1].reshape(-1, heads, hdim)
        return jnp.einsum(
            "hqk,khd->hqd",
            weights.astype(jnp.bfloat16),
            v_heads,
            preferred_element_type=jnp.float32,
        )

    def absorb(state, pair, key_img):

        def update(carry):
            running_max, running_sum, accum = carry
            scores = masked_scores(pair, key_img)
            new_max = jnp.maximum(running_max, jnp.max(scores, axis=2, keepdims=True))
            factor = jnp.exp(running_max - new_max)
            weights = jnp.exp(scores - new_max)
            new_sum = running_sum * factor + jnp.sum(weights, axis=2, keepdims=True)
            new_accum = accum * factor + weigh_values(weights, pair)
            return (new_max, new_sum, new_accum)

        live = jnp.logical_and(
            jnp.max(key_img) >= jnp.maximum(jnp.min(query_img), 0),
            jnp.min(jnp.where(key_img >= 0, key_img, 1 << 30)) <= jnp.max(query_img),
        )
        return lax.cond(live, update, lambda carry: carry, state)

    first_scores = masked_scores(own_pair, query_img)
    first_max = jnp.max(first_scores, axis=2, keepdims=True)
    first_weights = jnp.exp(first_scores - first_max)
    state = (
        first_max,
        jnp.sum(first_weights, axis=2, keepdims=True),
        weigh_values(first_weights, own_pair),
    )
    from_left = own_pair
    from_right = own_pair
    for step in range(1, reach + 1):
        from_left = passed_along(from_left, BLK, 1)
        from_right = passed_along(from_right, BLK, -1)
        state = absorb(state, from_left, token_images(me_index - step))
        state = absorb(state, from_right, token_images(me_index + step))
    heads_out = state[2] / state[1]
    attended = heads_out.transpose(1, 0, 2).reshape(tok, width).astype(jnp.bfloat16)
    stream = residual_in.astype(jnp.float32) + jnp.dot(
        attended, out_proj, preferred_element_type=jnp.float32
    )
    normed = layer_norm(stream, ln_gain).astype(jnp.bfloat16)
    merged = normed.reshape(row_count, 4 * width)
    feat = merge_proj.shape[0]
    out_width = merge_proj.shape[1]
    half = out_width // cores
    core_index = lax.axis_index("core")
    chip_index = lax.axis_index("chip")
    chip_weights = lax.all_to_all(merge_proj, "core", split_axis=1, concat_axis=0, tiled=True)
    by_chip = lax.all_to_all(
        merged.reshape(row_count, chips, cores * feat), "chip", split_axis=1, concat_axis=0, tiled=True
    )
    chip_rows = lax.all_gather(
        by_chip.reshape(chips, 1, row_count, cores * feat), "core", axis=1, tiled=True
    ).reshape(
        chips * cores * row_count, cores * feat
    )
    partial = jnp.dot(chip_rows, chip_weights, preferred_element_type=jnp.float32).astype(jnp.bfloat16)
    projected = lax.psum_scatter(partial, "chip", scatter_dimension=0, tiled=True).astype(jnp.float32)
    pair_rows = cores * row_count
    rows = chip_index * pair_rows + jnp.arange(pair_rows, dtype=jnp.int32)
    my_rows_img = jnp.sum((rows[:, None] >= ends[None, :]).astype(jnp.int32), axis=1)
    nimg = image_rows.shape[0]
    member = (my_rows_img[:, None] == jnp.arange(nimg, dtype=jnp.int32)[None, :]).astype(
        jnp.float32
    )
    row_squares = jnp.sum(projected * projected, axis=1)
    local_sums = jnp.sum(member * row_squares[:, None], axis=0)
    spread = jnp.broadcast_to(local_sums[None, :], (blocks, nimg))
    image_sums = jnp.sum(lax.all_to_all(spread, BLK, split_axis=0, concat_axis=0, tiled=True), axis=0)
    image_mean = image_sums / (image_rows.astype(jnp.float32) * out_width)
    row_scale = jnp.sum(member * lax.rsqrt(image_mean + 1e-06)[None, :], axis=1)
    my_gain = lax.dynamic_slice_in_dim(out_gain, core_index * half, half)
    scaled = (projected * row_scale[:, None] * my_gain[None, :]).astype(jnp.bfloat16)
    capacity = max(2, 2 * row_count // blocks)
    owner = lax.all_to_all(
        jnp.broadcast_to(owners[:, 0][None, :], (cores, row_count)),
        "core",
        split_axis=0,
        concat_axis=0,
        tiled=True,
    )
    onehot = (owner[:, :, None] == jnp.arange(blocks, dtype=jnp.int32)[None, None, :]).astype(jnp.int32)
    rank = jnp.sum(jnp.cumsum(onehot, axis=1) * onehot, axis=2) - 1
    slot = (
        owner * (cores * capacity)
        + jnp.arange(cores, dtype=jnp.int32)[:, None] * capacity
        + rank
    ).reshape(pair_rows)
    placement = (
        jnp.arange(blocks * cores * capacity, dtype=jnp.int32)[:, None] == slot[None, :]
    ).astype(jnp.bfloat16)
    outgoing = jnp.dot(placement, scaled, preferred_element_type=jnp.float32).astype(jnp.bfloat16)
    incoming = lax.all_to_all(outgoing, BLK, split_axis=0, concat_axis=0, tiled=True)
    return (
        incoming.reshape(chips, cores, cores, capacity, half)
        .transpose(0, 2, 3, 1, 4)
        .reshape(blocks * capacity, out_width)
    )


def solution(mesh):
    devices = mesh.devices
    cores = 2
    split_mesh = jax.sharding.Mesh(
        devices.reshape(devices.shape[0], devices.shape[1] // cores, cores), ("dp", "chip", "core")
    )
    rows = P(("dp", "chip", "core"), None)
    in_specs = (rows, rows, rows, rows, P(), P(), P(("chip", "core"), None), P(), P("dp"), rows)
    return jax.shard_map(on_device, mesh=split_mesh, in_specs=in_specs, out_specs=rows, check_vma=False)
```

```python
import jax
import jax.numpy as jnp
from jax import lax
from jax.sharding import PartitionSpec as P

HEADS = 16


BLK = ("zo", "zi", "x", "core")
GROUP = ("zi", "core")
OTHER = ("zo", "x")


def passed_along(value, axis, steps):
    count = lax.axis_size(BLK)
    first, last = (max(0, -steps), min(count, count - steps))
    return lax.ppermute(value, axis, [(source, source + steps) for source in range(first, last)])


def layer_norm(stream, gain):
    mean = jnp.mean(stream, axis=1, keepdims=True)
    centred = stream - mean
    var = jnp.mean(centred * centred, axis=1, keepdims=True)
    return centred * lax.rsqrt(var + 1e-06) * gain[None, :]


def on_device(
    queries, keys, values, residual_in, out_proj, ln_gain, merge_proj, out_gain, image_rows, owners
):
    blocks = lax.axis_size(BLK)
    me_index = lax.axis_index(BLK)
    tok, width = queries.shape
    row_count = tok // 4
    heads = HEADS
    hdim = width // heads
    reach = min(6, (blocks - 1) // 2)
    scale = 1.0 / hdim**0.5
    ends = jnp.cumsum(image_rows)

    def token_images(source):
        rows = source * row_count + jnp.arange(tok, dtype=jnp.int32) // 4
        found = jnp.sum((rows[:, None] >= ends[None, :]).astype(jnp.int32), axis=1)
        inside = jnp.logical_and(source >= 0, source < blocks)
        return jnp.where(inside, found, -1)

    query_img = token_images(me_index)
    q_heads = queries.reshape(tok, heads, hdim)
    own_pair = jnp.stack([keys, values])

    def masked_scores(pair, key_img):
        k_heads = pair[0].reshape(-1, heads, hdim)
        scores = (
            jnp.einsum("qhd,khd->hqk", q_heads, k_heads, preferred_element_type=jnp.float32) * scale
        )
        return jnp.where(query_img[None, :, None] == key_img[None, None, :], scores, -jnp.inf)

    def weigh_values(weights, pair):
        v_heads = pair[1].reshape(-1, heads, hdim)
        return jnp.einsum(
            "hqk,khd->hqd",
            weights.astype(jnp.bfloat16),
            v_heads,
            preferred_element_type=jnp.float32,
        )

    def absorb(state, pair, key_img):

        def update(carry):
            running_max, running_sum, accum = carry
            scores = masked_scores(pair, key_img)
            new_max = jnp.maximum(running_max, jnp.max(scores, axis=2, keepdims=True))
            factor = jnp.exp(running_max - new_max)
            weights = jnp.exp(scores - new_max)
            new_sum = running_sum * factor + jnp.sum(weights, axis=2, keepdims=True)
            new_accum = accum * factor + weigh_values(weights, pair)
            return (new_max, new_sum, new_accum)

        live = jnp.logical_and(
            jnp.max(key_img) >= jnp.maximum(jnp.min(query_img), 0),
            jnp.min(jnp.where(key_img >= 0, key_img, 1 << 30)) <= jnp.max(query_img),
        )
        return lax.cond(live, update, lambda carry: carry, state)

    first_scores = masked_scores(own_pair, query_img)
    first_max = jnp.max(first_scores, axis=2, keepdims=True)
    first_weights = jnp.exp(first_scores - first_max)
    state = (
        first_max,
        jnp.sum(first_weights, axis=2, keepdims=True),
        weigh_values(first_weights, own_pair),
    )
    from_left = own_pair
    from_right = own_pair
    for step in range(1, reach + 1):
        from_left = passed_along(from_left, BLK, 1)
        from_right = passed_along(from_right, BLK, -1)
        state = absorb(state, from_left, token_images(me_index - step))
        state = absorb(state, from_right, token_images(me_index + step))
    heads_out = state[2] / state[1]
    attended = heads_out.transpose(1, 0, 2).reshape(tok, width).astype(jnp.bfloat16)
    stream = residual_in.astype(jnp.float32) + jnp.dot(
        attended, out_proj, preferred_element_type=jnp.float32
    )
    normed = layer_norm(stream, ln_gain).astype(jnp.bfloat16)
    merged = normed.reshape(row_count, 4 * width)
    feat = merge_proj.shape[0]
    out_width = merge_proj.shape[1]
    n_zo, n_zi, n_x, n_core = (lax.axis_size(name) for name in BLK)
    group = n_zi * n_core
    others = n_zo * n_x
    part = out_width // group
    group_index = lax.axis_index(GROUP)
    other_index = lax.axis_index(OTHER)
    group_weights = lax.all_to_all(merge_proj, GROUP, split_axis=1, concat_axis=0, tiled=True)
    by_group = (
        merged.reshape(row_count, n_zo, n_zi, n_x, n_core, feat)
        .transpose(0, 1, 3, 2, 4, 5)
        .reshape(row_count, others, group * feat)
    )
    by_other = lax.all_to_all(by_group, OTHER, split_axis=1, concat_axis=0, tiled=True)
    group_rows = lax.all_gather(
        by_other.reshape(others, 1, row_count, group * feat), GROUP, axis=1, tiled=True
    ).reshape(others * group * row_count, group * feat)
    partial = jnp.dot(group_rows, group_weights, preferred_element_type=jnp.float32).astype(
        jnp.bfloat16
    )
    projected = lax.psum_scatter(partial, OTHER, scatter_dimension=0, tiled=True).astype(
        jnp.float32
    )
    zo_index = other_index // n_x
    x_index = other_index % n_x
    member_blocks = (
        zo_index * (n_zi * n_x * n_core)
        + (jnp.arange(group, dtype=jnp.int32) // n_core) * (n_x * n_core)
        + x_index * n_core
        + jnp.arange(group, dtype=jnp.int32) % n_core
    )
    rows = (member_blocks[:, None] * row_count + jnp.arange(row_count, dtype=jnp.int32)[None, :]).reshape(
        group * row_count
    )
    my_rows_img = jnp.sum((rows[:, None] >= ends[None, :]).astype(jnp.int32), axis=1)
    nimg = image_rows.shape[0]
    member = (my_rows_img[:, None] == jnp.arange(nimg, dtype=jnp.int32)[None, :]).astype(
        jnp.float32
    )
    row_squares = jnp.sum(projected * projected, axis=1)
    local_sums = jnp.sum(member * row_squares[:, None], axis=0)
    spread = jnp.broadcast_to(local_sums[None, :], (blocks, nimg))
    image_sums = jnp.sum(lax.all_to_all(spread, BLK, split_axis=0, concat_axis=0, tiled=True), axis=0)
    image_mean = image_sums / (image_rows.astype(jnp.float32) * out_width)
    row_scale = jnp.sum(member * lax.rsqrt(image_mean + 1e-06)[None, :], axis=1)
    my_gain = lax.dynamic_slice_in_dim(out_gain, group_index * part, part)
    scaled = (projected * row_scale[:, None] * my_gain[None, :]).astype(jnp.bfloat16)
    capacity = max(2, 2 * row_count // blocks)
    owner = lax.all_to_all(
        jnp.broadcast_to(owners[:, 0][None, :], (group, row_count)),
        GROUP,
        split_axis=0,
        concat_axis=0,
        tiled=True,
    )
    onehot = (owner[:, :, None] == jnp.arange(blocks, dtype=jnp.int32)[None, None, :]).astype(jnp.int32)
    rank = jnp.sum(jnp.cumsum(onehot, axis=1) * onehot, axis=2) - 1
    slot = (
        owner * (group * capacity) + jnp.arange(group, dtype=jnp.int32)[:, None] * capacity + rank
    ).reshape(group * row_count)
    placement = (
        jnp.arange(blocks * group * capacity, dtype=jnp.int32)[:, None] == slot[None, :]
    ).astype(jnp.bfloat16)
    outgoing = jnp.dot(placement, scaled, preferred_element_type=jnp.float32).astype(jnp.bfloat16)
    incoming = lax.all_to_all(outgoing, BLK, split_axis=0, concat_axis=0, tiled=True)
    return (
        incoming.reshape(n_zo, n_zi, n_x, n_core, n_zi, n_core, capacity, part)
        .transpose(0, 4, 2, 5, 6, 1, 3, 7)
        .reshape(blocks * capacity, out_width)
    )


def solution(mesh):
    devices = mesh.devices
    n_dp, n_blk = devices.shape
    split_mesh = jax.sharding.Mesh(
        devices.reshape(n_dp, 2, 2, n_blk // 8, 2), ("dp",) + BLK
    )
    rows = P(("dp",) + BLK, None)
    in_specs = (rows, rows, rows, rows, P(), P(), P(BLK, None), P(), P("dp"), rows)
    return jax.shard_map(
        on_device, mesh=split_mesh, in_specs=in_specs, out_specs=rows, check_vma=False
    )
```

```python
import jax
import jax.numpy as jnp
from jax import lax
from jax.sharding import PartitionSpec as P

HEADS = 16


BLK = ("chip", "core")


def passed_along(value, axis, steps):
    count = lax.axis_size("chip") * lax.axis_size("core")
    first, last = (max(0, -steps), min(count, count - steps))
    return lax.ppermute(value, axis, [(source, source + steps) for source in range(first, last)])


def layer_norm(stream, gain):
    mean = jnp.mean(stream, axis=1, keepdims=True)
    centred = stream - mean
    var = jnp.mean(centred * centred, axis=1, keepdims=True)
    return centred * lax.rsqrt(var + 1e-06) * gain[None, :]


def on_device(
    queries, keys, values, residual_in, out_proj, ln_gain, merge_proj, out_gain, image_rows, owners
):
    chips = lax.axis_size("chip")
    cores = lax.axis_size("core")
    blocks = chips * cores
    me_index = lax.axis_index("chip") * cores + lax.axis_index("core")
    tok, width = queries.shape
    row_count = tok // 4
    heads = HEADS
    hdim = width // heads
    reach = min(6, (blocks - 1) // 2)
    scale = 1.0 / hdim**0.5
    ends = jnp.cumsum(image_rows)

    def token_images(source):
        rows = source * row_count + jnp.arange(tok, dtype=jnp.int32) // 4
        found = jnp.sum((rows[:, None] >= ends[None, :]).astype(jnp.int32), axis=1)
        inside = jnp.logical_and(source >= 0, source < blocks)
        return jnp.where(inside, found, -1)

    query_img = token_images(me_index)
    q_heads = queries.reshape(tok, heads, hdim)
    own_pair = jnp.stack([keys, values])

    def masked_scores(pair, key_img):
        k_heads = pair[0].reshape(-1, heads, hdim)
        scores = (
            jnp.einsum("qhd,khd->hqk", q_heads, k_heads, preferred_element_type=jnp.float32) * scale
        )
        return jnp.where(query_img[None, :, None] == key_img[None, None, :], scores, -jnp.inf)

    def weigh_values(weights, pair):
        v_heads = pair[1].reshape(-1, heads, hdim)
        return jnp.einsum(
            "hqk,khd->hqd",
            weights.astype(jnp.bfloat16),
            v_heads,
            preferred_element_type=jnp.float32,
        )

    def absorb(state, pair, key_img):

        def update(carry):
            running_max, running_sum, accum = carry
            scores = masked_scores(pair, key_img)
            new_max = jnp.maximum(running_max, jnp.max(scores, axis=2, keepdims=True))
            factor = jnp.exp(running_max - new_max)
            weights = jnp.exp(scores - new_max)
            new_sum = running_sum * factor + jnp.sum(weights, axis=2, keepdims=True)
            new_accum = accum * factor + weigh_values(weights, pair)
            return (new_max, new_sum, new_accum)

        live = jnp.logical_and(
            jnp.max(key_img) >= jnp.maximum(jnp.min(query_img), 0),
            jnp.min(jnp.where(key_img >= 0, key_img, 1 << 30)) <= jnp.max(query_img),
        )
        return lax.cond(live, update, lambda carry: carry, state)

    first_scores = masked_scores(own_pair, query_img)
    first_max = jnp.max(first_scores, axis=2, keepdims=True)
    first_weights = jnp.exp(first_scores - first_max)
    state = (
        first_max,
        jnp.sum(first_weights, axis=2, keepdims=True),
        weigh_values(first_weights, own_pair),
    )
    from_left = own_pair
    from_right = own_pair
    for step in range(1, reach + 1):
        from_left = passed_along(from_left, BLK, 1)
        from_right = passed_along(from_right, BLK, -1)
        state = absorb(state, from_left, token_images(me_index - step))
        state = absorb(state, from_right, token_images(me_index + step))
    heads_out = state[2] / state[1]
    attended = heads_out.transpose(1, 0, 2).reshape(tok, width).astype(jnp.bfloat16)
    stream = residual_in.astype(jnp.float32) + jnp.dot(
        attended, out_proj, preferred_element_type=jnp.float32
    )
    normed = layer_norm(stream, ln_gain).astype(jnp.bfloat16)
    merged = normed.reshape(row_count, 4 * width)
    feat = merge_proj.shape[0]
    out_width = merge_proj.shape[1]
    half = out_width // cores
    core_index = lax.axis_index("core")
    chip_index = lax.axis_index("chip")
    chip_weights = lax.all_to_all(merge_proj, "core", split_axis=1, concat_axis=0, tiled=True)
    by_chip = lax.all_to_all(
        merged.reshape(row_count, chips, cores * feat), "chip", split_axis=1, concat_axis=0, tiled=True
    )
    chip_rows = lax.all_gather(
        by_chip.reshape(chips, 1, row_count, cores * feat), "core", axis=1, tiled=True
    ).reshape(
        chips * cores * row_count, cores * feat
    )
    partial = jnp.dot(chip_rows, chip_weights, preferred_element_type=jnp.float32).astype(jnp.bfloat16)
    projected = jnp.sum(
        lax.all_to_all(
            partial.reshape(chips, -1, partial.shape[1]), "chip", split_axis=0, concat_axis=0, tiled=True
        ).astype(jnp.float32),
        axis=0,
    )
    pair_rows = cores * row_count
    rows = chip_index * pair_rows + jnp.arange(pair_rows, dtype=jnp.int32)
    my_rows_img = jnp.sum((rows[:, None] >= ends[None, :]).astype(jnp.int32), axis=1)
    nimg = image_rows.shape[0]
    member = (my_rows_img[:, None] == jnp.arange(nimg, dtype=jnp.int32)[None, :]).astype(
        jnp.float32
    )
    row_squares = jnp.sum(projected * projected, axis=1)
    local_sums = jnp.sum(member * row_squares[:, None], axis=0)
    spread = jnp.broadcast_to(local_sums[None, :], (blocks, nimg))
    image_sums = jnp.sum(lax.all_to_all(spread, BLK, split_axis=0, concat_axis=0, tiled=True), axis=0)
    image_mean = image_sums / (image_rows.astype(jnp.float32) * out_width)
    row_scale = jnp.sum(member * lax.rsqrt(image_mean + 1e-06)[None, :], axis=1)
    my_gain = lax.dynamic_slice_in_dim(out_gain, core_index * half, half)
    scaled = (projected * row_scale[:, None] * my_gain[None, :]).astype(jnp.bfloat16)
    capacity = max(2, 2 * row_count // blocks)
    owner = lax.all_to_all(
        jnp.broadcast_to(owners[:, 0][None, :], (cores, row_count)),
        "core",
        split_axis=0,
        concat_axis=0,
        tiled=True,
    )
    onehot = (owner[:, :, None] == jnp.arange(blocks, dtype=jnp.int32)[None, None, :]).astype(jnp.int32)
    rank = jnp.sum(jnp.cumsum(onehot, axis=1) * onehot, axis=2) - 1
    slot = (
        owner * (cores * capacity)
        + jnp.arange(cores, dtype=jnp.int32)[:, None] * capacity
        + rank
    ).reshape(pair_rows)
    placement = (
        jnp.arange(blocks * cores * capacity, dtype=jnp.int32)[:, None] == slot[None, :]
    ).astype(jnp.bfloat16)
    outgoing = jnp.dot(placement, scaled, preferred_element_type=jnp.float32).astype(jnp.bfloat16)
    incoming = lax.all_to_all(outgoing, BLK, split_axis=0, concat_axis=0, tiled=True)
    return (
        incoming.reshape(chips, cores, cores, capacity, half)
        .transpose(0, 2, 3, 1, 4)
        .reshape(blocks * capacity, out_width)
    )


def solution(mesh):
    devices = mesh.devices
    cores = 2
    split_mesh = jax.sharding.Mesh(
        devices.reshape(devices.shape[0], devices.shape[1] // cores, cores), ("dp", "chip", "core")
    )
    rows = P(("dp", "chip", "core"), None)
    in_specs = (rows, rows, rows, rows, P(), P(), P(("chip", "core"), None), P(), P("dp"), rows)
    return jax.shard_map(on_device, mesh=split_mesh, in_specs=in_specs, out_specs=rows, check_vma=False)
```

```python
import jax
import jax.numpy as jnp
from jax import lax
from jax.sharding import PartitionSpec as P

HEADS = 16


BLK = ("chip", "core")


def passed_along(value, axis, steps):
    count = lax.axis_size("chip") * lax.axis_size("core")
    first, last = (max(0, -steps), min(count, count - steps))
    return lax.ppermute(value, axis, [(source, source + steps) for source in range(first, last)])


def layer_norm(stream, gain):
    mean = jnp.mean(stream, axis=1, keepdims=True)
    centred = stream - mean
    var = jnp.mean(centred * centred, axis=1, keepdims=True)
    return centred * lax.rsqrt(var + 1e-06) * gain[None, :]


def on_device(
    queries, keys, values, residual_in, out_proj, ln_gain, merge_proj, out_gain, image_rows, owners
):
    chips = lax.axis_size("chip")
    cores = lax.axis_size("core")
    blocks = chips * cores
    me_index = lax.axis_index("chip") * cores + lax.axis_index("core")
    tok, width = queries.shape
    row_count = tok // 4
    heads = HEADS
    hdim = width // heads
    reach = min(6, (blocks - 1) // 2)
    scale = 1.0 / hdim**0.5
    ends = jnp.cumsum(image_rows)

    def token_images(source):
        rows = source * row_count + jnp.arange(tok, dtype=jnp.int32) // 4
        found = jnp.sum((rows[:, None] >= ends[None, :]).astype(jnp.int32), axis=1)
        inside = jnp.logical_and(source >= 0, source < blocks)
        return jnp.where(inside, found, -1)

    query_img = token_images(me_index)
    q_heads = queries.reshape(tok, heads, hdim)
    own_pair = jnp.stack([keys, values])

    def masked_scores(pair, key_img):
        k_heads = pair[0].reshape(-1, heads, hdim)
        scores = (
            jnp.einsum("qhd,khd->hqk", q_heads, k_heads, preferred_element_type=jnp.float32) * scale
        )
        return jnp.where(query_img[None, :, None] == key_img[None, None, :], scores, -jnp.inf)

    def weigh_values(weights, pair):
        v_heads = pair[1].reshape(-1, heads, hdim)
        return jnp.einsum(
            "hqk,khd->hqd",
            weights.astype(jnp.bfloat16),
            v_heads,
            preferred_element_type=jnp.float32,
        )

    def absorb(state, pair, key_img):

        def update(carry):
            running_max, running_sum, accum = carry
            scores = masked_scores(pair, key_img)
            new_max = jnp.maximum(running_max, jnp.max(scores, axis=2, keepdims=True))
            factor = jnp.exp(running_max - new_max)
            weights = jnp.exp(scores - new_max)
            new_sum = running_sum * factor + jnp.sum(weights, axis=2, keepdims=True)
            new_accum = accum * factor + weigh_values(weights, pair)
            return (new_max, new_sum, new_accum)

        live = jnp.logical_and(
            jnp.max(key_img) >= jnp.maximum(jnp.min(query_img), 0),
            jnp.min(jnp.where(key_img >= 0, key_img, 1 << 30)) <= jnp.max(query_img),
        )
        return lax.cond(live, update, lambda carry: carry, state)

    first_scores = masked_scores(own_pair, query_img)
    first_max = jnp.max(first_scores, axis=2, keepdims=True)
    first_weights = jnp.exp(first_scores - first_max)
    state = (
        first_max,
        jnp.sum(first_weights, axis=2, keepdims=True),
        weigh_values(first_weights, own_pair),
    )
    from_left = own_pair
    from_right = own_pair
    for step in range(1, reach + 1):
        from_left = passed_along(from_left, BLK, 1)
        from_right = passed_along(from_right, BLK, -1)
        state = absorb(state, from_left, token_images(me_index - step))
        state = absorb(state, from_right, token_images(me_index + step))
    heads_out = state[2] / state[1]
    attended = heads_out.transpose(1, 0, 2).reshape(tok, width).astype(jnp.bfloat16)
    stream = residual_in.astype(jnp.float32) + jnp.dot(
        attended, out_proj, preferred_element_type=jnp.float32
    )
    normed = layer_norm(stream, ln_gain).astype(jnp.bfloat16)
    merged = normed.reshape(row_count, 4 * width)
    feat = merge_proj.shape[0]
    out_width = merge_proj.shape[1]
    half = out_width // cores
    core_index = lax.axis_index("core")
    chip_index = lax.axis_index("chip")
    chip_weights = lax.all_to_all(merge_proj, "core", split_axis=1, concat_axis=0, tiled=True)
    by_device = jnp.broadcast_to(
        merged.reshape(row_count, chips, 1, cores * feat), (row_count, chips, cores, cores * feat)
    ).reshape(row_count, blocks, cores * feat)
    chip_rows = lax.all_to_all(by_device, BLK, split_axis=1, concat_axis=0, tiled=True).reshape(
        blocks * row_count, cores * feat
    )
    partial = jnp.dot(chip_rows, chip_weights, preferred_element_type=jnp.float32).astype(jnp.bfloat16)
    projected = lax.psum_scatter(partial, "chip", scatter_dimension=0, tiled=True).astype(jnp.float32)
    pair_rows = cores * row_count
    rows = chip_index * pair_rows + jnp.arange(pair_rows, dtype=jnp.int32)
    my_rows_img = jnp.sum((rows[:, None] >= ends[None, :]).astype(jnp.int32), axis=1)
    nimg = image_rows.shape[0]
    member = (my_rows_img[:, None] == jnp.arange(nimg, dtype=jnp.int32)[None, :]).astype(
        jnp.float32
    )
    row_squares = jnp.sum(projected * projected, axis=1)
    local_sums = jnp.sum(member * row_squares[:, None], axis=0)
    spread = jnp.broadcast_to(local_sums[None, :], (blocks, nimg))
    image_sums = jnp.sum(lax.all_to_all(spread, BLK, split_axis=0, concat_axis=0, tiled=True), axis=0)
    image_mean = image_sums / (image_rows.astype(jnp.float32) * out_width)
    row_scale = jnp.sum(member * lax.rsqrt(image_mean + 1e-06)[None, :], axis=1)
    my_gain = lax.dynamic_slice_in_dim(out_gain, core_index * half, half)
    scaled = (projected * row_scale[:, None] * my_gain[None, :]).astype(jnp.bfloat16)
    capacity = max(2, 2 * row_count // blocks)
    owner = lax.all_to_all(
        jnp.broadcast_to(owners[:, 0][None, :], (cores, row_count)),
        "core",
        split_axis=0,
        concat_axis=0,
        tiled=True,
    )
    onehot = (owner[:, :, None] == jnp.arange(blocks, dtype=jnp.int32)[None, None, :]).astype(jnp.int32)
    rank = jnp.sum(jnp.cumsum(onehot, axis=1) * onehot, axis=2) - 1
    slot = (
        owner * (cores * capacity)
        + jnp.arange(cores, dtype=jnp.int32)[:, None] * capacity
        + rank
    ).reshape(pair_rows)
    placement = (
        jnp.arange(blocks * cores * capacity, dtype=jnp.int32)[:, None] == slot[None, :]
    ).astype(jnp.bfloat16)
    outgoing = jnp.dot(placement, scaled, preferred_element_type=jnp.float32).astype(jnp.bfloat16)
    incoming = lax.all_to_all(outgoing, BLK, split_axis=0, concat_axis=0, tiled=True)
    return (
        incoming.reshape(chips, cores, cores, capacity, half)
        .transpose(0, 2, 3, 1, 4)
        .reshape(blocks * capacity, out_width)
    )


def solution(mesh):
    devices = mesh.devices
    cores = 2
    split_mesh = jax.sharding.Mesh(
        devices.reshape(devices.shape[0], devices.shape[1] // cores, cores), ("dp", "chip", "core")
    )
    rows = P(("dp", "chip", "core"), None)
    in_specs = (rows, rows, rows, rows, P(), P(), P(("chip", "core"), None), P(), P("dp"), rows)
    return jax.shard_map(on_device, mesh=split_mesh, in_specs=in_specs, out_specs=rows, check_vma=False)
```

```python
import jax
import jax.numpy as jnp
from jax import lax
from jax.sharding import PartitionSpec as P

HEADS = 16


BLK = ("chip", "core")


def passed_along(value, axis, steps):
    count = lax.axis_size("chip") * lax.axis_size("core")
    first, last = (max(0, -steps), min(count, count - steps))
    return lax.ppermute(value, axis, [(source, source + steps) for source in range(first, last)])


def layer_norm(stream, gain):
    mean = jnp.mean(stream, axis=1, keepdims=True)
    centred = stream - mean
    var = jnp.mean(centred * centred, axis=1, keepdims=True)
    return centred * lax.rsqrt(var + 1e-06) * gain[None, :]


def on_device(
    queries, keys, values, residual_in, out_proj, ln_gain, merge_proj, out_gain, image_rows, owners
):
    chips = lax.axis_size("chip")
    cores = lax.axis_size("core")
    blocks = chips * cores
    me_index = lax.axis_index("chip") * cores + lax.axis_index("core")
    tok, width = queries.shape
    row_count = tok // 4
    heads = HEADS
    hdim = width // heads
    reach = min(6, (blocks - 1) // 2)
    scale = 1.0 / hdim**0.5
    ends = jnp.cumsum(image_rows)

    def token_images(source):
        rows = source * row_count + jnp.arange(tok, dtype=jnp.int32) // 4
        found = jnp.sum((rows[:, None] >= ends[None, :]).astype(jnp.int32), axis=1)
        inside = jnp.logical_and(source >= 0, source < blocks)
        return jnp.where(inside, found, -1)

    query_img = token_images(me_index)
    q_heads = queries.reshape(tok, heads, hdim)
    own_pair = (keys, values)

    def masked_scores(pair, key_img):
        k_heads = pair[0].reshape(-1, heads, hdim)
        scores = (
            jnp.einsum("qhd,khd->hqk", q_heads, k_heads, preferred_element_type=jnp.float32) * scale
        )
        return jnp.where(query_img[None, :, None] == key_img[None, None, :], scores, -jnp.inf)

    def weigh_values(weights, pair):
        v_heads = pair[1].reshape(-1, heads, hdim)
        return jnp.einsum(
            "hqk,khd->hqd",
            weights.astype(jnp.bfloat16),
            v_heads,
            preferred_element_type=jnp.float32,
        )

    def absorb(state, pair, key_img):

        def update(carry):
            running_max, running_sum, accum = carry
            scores = masked_scores(pair, key_img)
            new_max = jnp.maximum(running_max, jnp.max(scores, axis=2, keepdims=True))
            factor = jnp.exp(running_max - new_max)
            weights = jnp.exp(scores - new_max)
            new_sum = running_sum * factor + jnp.sum(weights, axis=2, keepdims=True)
            new_accum = accum * factor + weigh_values(weights, pair)
            return (new_max, new_sum, new_accum)

        live = jnp.logical_and(
            jnp.max(key_img) >= jnp.maximum(jnp.min(query_img), 0),
            jnp.min(jnp.where(key_img >= 0, key_img, 1 << 30)) <= jnp.max(query_img),
        )
        return lax.cond(live, update, lambda carry: carry, state)

    first_scores = masked_scores(own_pair, query_img)
    first_max = jnp.max(first_scores, axis=2, keepdims=True)
    first_weights = jnp.exp(first_scores - first_max)
    state = (
        first_max,
        jnp.sum(first_weights, axis=2, keepdims=True),
        weigh_values(first_weights, own_pair),
    )
    from_left = own_pair
    from_right = own_pair
    for step in range(1, reach + 1):
        from_left = tuple(passed_along(x, BLK, 1) for x in from_left)
        from_right = tuple(passed_along(x, BLK, -1) for x in from_right)
        state = absorb(state, from_left, token_images(me_index - step))
        state = absorb(state, from_right, token_images(me_index + step))
    heads_out = state[2] / state[1]
    attended = heads_out.transpose(1, 0, 2).reshape(tok, width).astype(jnp.bfloat16)
    stream = residual_in.astype(jnp.float32) + jnp.dot(
        attended, out_proj, preferred_element_type=jnp.float32
    )
    normed = layer_norm(stream, ln_gain).astype(jnp.bfloat16)
    merged = normed.reshape(row_count, 4 * width)
    feat = merge_proj.shape[0]
    out_width = merge_proj.shape[1]
    half = out_width // cores
    core_index = lax.axis_index("core")
    chip_index = lax.axis_index("chip")
    chip_weights = lax.all_to_all(merge_proj, "core", split_axis=1, concat_axis=0, tiled=True)
    by_device = jnp.broadcast_to(
        merged.reshape(row_count, chips, 1, cores * feat), (row_count, chips, cores, cores * feat)
    ).reshape(row_count, blocks, cores * feat)
    chip_rows = lax.all_to_all(by_device, BLK, split_axis=1, concat_axis=0, tiled=True).reshape(
        blocks * row_count, cores * feat
    )
    partial = jnp.dot(chip_rows, chip_weights, preferred_element_type=jnp.float32).astype(jnp.bfloat16)
    projected = lax.psum_scatter(partial, "chip", scatter_dimension=0, tiled=True).astype(jnp.float32)
    pair_rows = cores * row_count
    rows = chip_index * pair_rows + jnp.arange(pair_rows, dtype=jnp.int32)
    my_rows_img = jnp.sum((rows[:, None] >= ends[None, :]).astype(jnp.int32), axis=1)
    nimg = image_rows.shape[0]
    member = (my_rows_img[:, None] == jnp.arange(nimg, dtype=jnp.int32)[None, :]).astype(
        jnp.float32
    )
    row_squares = jnp.sum(projected * projected, axis=1)
    local_sums = jnp.sum(member * row_squares[:, None], axis=0)
    spread = jnp.broadcast_to(local_sums[None, :], (blocks, nimg))
    image_sums = jnp.sum(lax.all_to_all(spread, BLK, split_axis=0, concat_axis=0, tiled=True), axis=0)
    image_mean = image_sums / (image_rows.astype(jnp.float32) * out_width)
    row_scale = jnp.sum(member * lax.rsqrt(image_mean + 1e-06)[None, :], axis=1)
    my_gain = lax.dynamic_slice_in_dim(out_gain, core_index * half, half)
    scaled = (projected * row_scale[:, None] * my_gain[None, :]).astype(jnp.bfloat16)
    capacity = max(2, 2 * row_count // blocks)
    owner = lax.all_to_all(
        jnp.broadcast_to(owners[:, 0][None, :], (cores, row_count)),
        "core",
        split_axis=0,
        concat_axis=0,
        tiled=True,
    )
    onehot = (owner[:, :, None] == jnp.arange(blocks, dtype=jnp.int32)[None, None, :]).astype(jnp.int32)
    rank = jnp.sum(jnp.cumsum(onehot, axis=1) * onehot, axis=2) - 1
    slot = (
        owner * (cores * capacity)
        + jnp.arange(cores, dtype=jnp.int32)[:, None] * capacity
        + rank
    ).reshape(pair_rows)
    placement = (
        jnp.arange(blocks * cores * capacity, dtype=jnp.int32)[:, None] == slot[None, :]
    ).astype(jnp.bfloat16)
    outgoing = jnp.dot(placement, scaled, preferred_element_type=jnp.float32).astype(jnp.bfloat16)
    incoming = lax.all_to_all(outgoing, BLK, split_axis=0, concat_axis=0, tiled=True)
    return (
        incoming.reshape(chips, cores, cores, capacity, half)
        .transpose(0, 2, 3, 1, 4)
        .reshape(blocks * capacity, out_width)
    )


def solution(mesh):
    devices = mesh.devices
    cores = 2
    split_mesh = jax.sharding.Mesh(
        devices.reshape(devices.shape[0], devices.shape[1] // cores, cores), ("dp", "chip", "core")
    )
    rows = P(("dp", "chip", "core"), None)
    in_specs = (rows, rows, rows, rows, P(), P(), P(("chip", "core"), None), P(), P("dp"), rows)
    return jax.shard_map(on_device, mesh=split_mesh, in_specs=in_specs, out_specs=rows, check_vma=False)
```

```python
import jax
import jax.numpy as jnp
from jax import lax
from jax.sharding import PartitionSpec as P

HEADS = 16


BLK = ("chip", "core")


def passed_along(value, axis, steps):
    count = lax.axis_size("chip") * lax.axis_size("core")
    first, last = (max(0, -steps), min(count, count - steps))
    return lax.ppermute(value, axis, [(source, source + steps) for source in range(first, last)])


def layer_norm(stream, gain):
    mean = jnp.mean(stream, axis=1, keepdims=True)
    centred = stream - mean
    var = jnp.mean(centred * centred, axis=1, keepdims=True)
    return centred * lax.rsqrt(var + 1e-06) * gain[None, :]


def on_device(
    queries, keys, values, residual_in, out_proj, ln_gain, merge_proj, out_gain, image_rows, owners
):
    chips = lax.axis_size("chip")
    cores = lax.axis_size("core")
    blocks = chips * cores
    me_index = lax.axis_index("chip") * cores + lax.axis_index("core")
    tok, width = queries.shape
    row_count = tok // 4
    heads = HEADS
    hdim = width // heads
    reach = min(6, (blocks - 1) // 2)
    scale = 1.0 / hdim**0.5
    ends = jnp.cumsum(image_rows)

    def token_images(source):
        rows = source * row_count + jnp.arange(tok, dtype=jnp.int32) // 4
        found = jnp.sum((rows[:, None] >= ends[None, :]).astype(jnp.int32), axis=1)
        inside = jnp.logical_and(source >= 0, source < blocks)
        return jnp.where(inside, found, -1)

    query_img = token_images(me_index)
    q_heads = queries.reshape(tok, heads, hdim)
    own_pair = jnp.stack([keys, values])
    all_owners = lax.all_to_all(
        jnp.broadcast_to(owners[:, 0][None, :], (blocks, owners.shape[0])),
        BLK,
        split_axis=0,
        concat_axis=0,
        tiled=True,
    )

    def masked_scores(pair, key_img):
        k_heads = pair[0].reshape(-1, heads, hdim)
        scores = (
            jnp.einsum("qhd,khd->hqk", q_heads, k_heads, preferred_element_type=jnp.float32) * scale
        )
        return jnp.where(query_img[None, :, None] == key_img[None, None, :], scores, -jnp.inf)

    def weigh_values(weights, pair):
        v_heads = pair[1].reshape(-1, heads, hdim)
        return jnp.einsum(
            "hqk,khd->hqd",
            weights.astype(jnp.bfloat16),
            v_heads,
            preferred_element_type=jnp.float32,
        )

    def absorb(state, pair, key_img):

        def update(carry):
            running_max, running_sum, accum = carry
            scores = masked_scores(pair, key_img)
            new_max = jnp.maximum(running_max, jnp.max(scores, axis=2, keepdims=True))
            factor = jnp.exp(running_max - new_max)
            weights = jnp.exp(scores - new_max)
            new_sum = running_sum * factor + jnp.sum(weights, axis=2, keepdims=True)
            new_accum = accum * factor + weigh_values(weights, pair)
            return (new_max, new_sum, new_accum)

        live = jnp.logical_and(
            jnp.max(key_img) >= jnp.maximum(jnp.min(query_img), 0),
            jnp.min(jnp.where(key_img >= 0, key_img, 1 << 30)) <= jnp.max(query_img),
        )
        return lax.cond(live, update, lambda carry: carry, state)

    first_scores = masked_scores(own_pair, query_img)
    first_max = jnp.max(first_scores, axis=2, keepdims=True)
    first_weights = jnp.exp(first_scores - first_max)
    state = (
        first_max,
        jnp.sum(first_weights, axis=2, keepdims=True),
        weigh_values(first_weights, own_pair),
    )
    from_left = own_pair
    from_right = own_pair
    for step in range(1, reach + 1):
        from_left = passed_along(from_left, BLK, 1)
        from_right = passed_along(from_right, BLK, -1)
        state = absorb(state, from_left, token_images(me_index - step))
        state = absorb(state, from_right, token_images(me_index + step))
    heads_out = state[2] / state[1]
    attended = heads_out.transpose(1, 0, 2).reshape(tok, width).astype(jnp.bfloat16)
    stream = residual_in.astype(jnp.float32) + jnp.dot(
        attended, out_proj, preferred_element_type=jnp.float32
    )
    normed = layer_norm(stream, ln_gain).astype(jnp.bfloat16)
    merged = normed.reshape(row_count, 4 * width)
    feat = merge_proj.shape[0]
    out_width = merge_proj.shape[1]
    half = out_width // cores
    chip_index = lax.axis_index("chip")
    chip_weights = lax.all_to_all(merge_proj, "core", split_axis=1, concat_axis=0, tiled=True)
    by_device = jnp.broadcast_to(
        merged.reshape(row_count, chips, 1, cores * feat), (row_count, chips, cores, cores * feat)
    ).reshape(row_count, blocks, cores * feat)
    chip_rows = lax.all_to_all(by_device, BLK, split_axis=1, concat_axis=0, tiled=True).reshape(
        blocks * row_count, cores * feat
    )
    partial = jnp.dot(chip_rows, chip_weights, preferred_element_type=jnp.float32).astype(jnp.bfloat16)
    projected = lax.psum_scatter(partial, "chip", scatter_dimension=0, tiled=True).astype(jnp.float32)
    pair_rows = cores * row_count
    rows = chip_index * pair_rows + jnp.arange(pair_rows, dtype=jnp.int32)
    my_rows_img = jnp.sum((rows[:, None] >= ends[None, :]).astype(jnp.int32), axis=1)
    nimg = image_rows.shape[0]
    member = (my_rows_img[:, None] == jnp.arange(nimg, dtype=jnp.int32)[None, :]).astype(
        jnp.float32
    )
    row_squares = jnp.sum(projected * projected, axis=1)
    local_sums = jnp.sum(member * row_squares[:, None], axis=0)
    spread = jnp.broadcast_to(local_sums[None, :], (blocks, nimg))
    image_sums = jnp.sum(lax.all_to_all(spread, BLK, split_axis=0, concat_axis=0, tiled=True), axis=0)
    image_mean = image_sums / (image_rows.astype(jnp.float32) * out_width)
    capacity = max(2, 2 * row_count // blocks)
    owner = lax.all_to_all(
        jnp.broadcast_to(owners[:, 0][None, :], (cores, row_count)),
        "core",
        split_axis=0,
        concat_axis=0,
        tiled=True,
    )
    onehot = (owner[:, :, None] == jnp.arange(blocks, dtype=jnp.int32)[None, None, :]).astype(jnp.int32)
    rank = jnp.sum(jnp.cumsum(onehot, axis=1) * onehot, axis=2) - 1
    slot = (
        owner * (cores * capacity)
        + jnp.arange(cores, dtype=jnp.int32)[:, None] * capacity
        + rank
    ).reshape(pair_rows)
    placement = (
        jnp.arange(blocks * cores * capacity, dtype=jnp.int32)[:, None] == slot[None, :]
    ).astype(jnp.bfloat16)
    outgoing = jnp.dot(
        placement, projected.astype(jnp.bfloat16), preferred_element_type=jnp.float32
    ).astype(jnp.bfloat16)
    incoming = lax.all_to_all(outgoing, BLK, split_axis=0, concat_axis=0, tiled=True)
    mine = (all_owners == me_index).astype(jnp.int32)
    ranks = jnp.cumsum(mine, axis=1) * mine - 1
    chosen = (
        ranks[:, None, :] == jnp.arange(capacity, dtype=jnp.int32)[None, :, None]
    ).astype(jnp.float32)
    all_rows = jnp.arange(blocks * row_count, dtype=jnp.int32)
    all_img = jnp.sum((all_rows[:, None] >= ends[None, :]).astype(jnp.int32), axis=1)
    all_member = (all_img[:, None] == jnp.arange(nimg, dtype=jnp.int32)[None, :]).astype(jnp.float32)
    all_scale = jnp.sum(all_member * lax.rsqrt(image_mean + 1e-06)[None, :], axis=1)
    slot_scale = jnp.sum(chosen * all_scale.reshape(blocks, 1, row_count), axis=2).reshape(
        blocks * capacity
    )
    arranged = (
        incoming.reshape(chips, cores, cores, capacity, half)
        .transpose(0, 2, 3, 1, 4)
        .reshape(blocks * capacity, cores, half)
        .astype(jnp.float32)
    )
    scaled = arranged * slot_scale[:, None, None] * out_gain.reshape(cores, half)[None, :, :]
    return scaled.astype(jnp.bfloat16).reshape(blocks * capacity, out_width)


def solution(mesh):
    devices = mesh.devices
    cores = 2
    split_mesh = jax.sharding.Mesh(
        devices.reshape(devices.shape[0], devices.shape[1] // cores, cores), ("dp", "chip", "core")
    )
    rows = P(("dp", "chip", "core"), None)
    in_specs = (rows, rows, rows, rows, P(), P(), P(("chip", "core"), None), P(), P("dp"), rows)
    return jax.shard_map(on_device, mesh=split_mesh, in_specs=in_specs, out_specs=rows, check_vma=False)
```

```python
import jax
import jax.numpy as jnp
from jax import lax
from jax.sharding import PartitionSpec as P

HEADS = 16


BLK = ("chip", "core")


def passed_along(value, axis, steps):
    count = lax.axis_size("chip") * lax.axis_size("core")
    first, last = (max(0, -steps), min(count, count - steps))
    return lax.ppermute(value, axis, [(source, source + steps) for source in range(first, last)])


def layer_norm(stream, gain):
    mean = jnp.mean(stream, axis=1, keepdims=True)
    centred = stream - mean
    var = jnp.mean(centred * centred, axis=1, keepdims=True)
    return centred * lax.rsqrt(var + 1e-06) * gain[None, :]


def on_device(
    queries, keys, values, residual_in, out_proj, ln_gain, merge_proj, out_gain, image_rows, owners
):
    chips = lax.axis_size("chip")
    cores = lax.axis_size("core")
    blocks = chips * cores
    me_index = lax.axis_index("chip") * cores + lax.axis_index("core")
    tok, width = queries.shape
    row_count = tok // 4
    heads = HEADS
    hdim = width // heads
    reach = min(6, (blocks - 1) // 2)
    scale = 1.0 / hdim**0.5
    ends = jnp.cumsum(image_rows)

    def token_images(source):
        rows = source * row_count + jnp.arange(tok, dtype=jnp.int32) // 4
        found = jnp.sum((rows[:, None] >= ends[None, :]).astype(jnp.int32), axis=1)
        inside = jnp.logical_and(source >= 0, source < blocks)
        return jnp.where(inside, found, -1)

    query_img = token_images(me_index)
    q_heads = queries.reshape(tok, heads, hdim)
    own_pair = jnp.stack([keys, values])
    owner_from_left = passed_along(owners[:, 0], BLK, 1)
    owner_from_right = passed_along(owners[:, 0], BLK, -1)

    def masked_scores(pair, key_img):
        k_heads = pair[0].reshape(-1, heads, hdim)
        scores = (
            jnp.einsum("qhd,khd->hqk", q_heads, k_heads, preferred_element_type=jnp.float32) * scale
        )
        return jnp.where(query_img[None, :, None] == key_img[None, None, :], scores, -jnp.inf)

    def weigh_values(weights, pair):
        v_heads = pair[1].reshape(-1, heads, hdim)
        return jnp.einsum(
            "hqk,khd->hqd",
            weights.astype(jnp.bfloat16),
            v_heads,
            preferred_element_type=jnp.float32,
        )

    def absorb(state, pair, key_img):

        def update(carry):
            running_max, running_sum, accum = carry
            scores = masked_scores(pair, key_img)
            new_max = jnp.maximum(running_max, jnp.max(scores, axis=2, keepdims=True))
            factor = jnp.exp(running_max - new_max)
            weights = jnp.exp(scores - new_max)
            new_sum = running_sum * factor + jnp.sum(weights, axis=2, keepdims=True)
            new_accum = accum * factor + weigh_values(weights, pair)
            return (new_max, new_sum, new_accum)

        live = jnp.logical_and(
            jnp.max(key_img) >= jnp.maximum(jnp.min(query_img), 0),
            jnp.min(jnp.where(key_img >= 0, key_img, 1 << 30)) <= jnp.max(query_img),
        )
        return lax.cond(live, update, lambda carry: carry, state)

    first_scores = masked_scores(own_pair, query_img)
    first_max = jnp.max(first_scores, axis=2, keepdims=True)
    first_weights = jnp.exp(first_scores - first_max)
    state = (
        first_max,
        jnp.sum(first_weights, axis=2, keepdims=True),
        weigh_values(first_weights, own_pair),
    )
    from_left = own_pair
    from_right = own_pair
    for step in range(1, reach + 1):
        from_left = passed_along(from_left, BLK, 1)
        from_right = passed_along(from_right, BLK, -1)
        state = absorb(state, from_left, token_images(me_index - step))
        state = absorb(state, from_right, token_images(me_index + step))
    heads_out = state[2] / state[1]
    attended = heads_out.transpose(1, 0, 2).reshape(tok, width).astype(jnp.bfloat16)
    stream = residual_in.astype(jnp.float32) + jnp.dot(
        attended, out_proj, preferred_element_type=jnp.float32
    )
    normed = layer_norm(stream, ln_gain).astype(jnp.bfloat16)
    merged = normed.reshape(row_count, 4 * width)
    feat = merge_proj.shape[0]
    out_width = merge_proj.shape[1]
    half = out_width // cores
    core_index = lax.axis_index("core")
    chip_index = lax.axis_index("chip")
    chip_weights = lax.all_to_all(merge_proj, "core", split_axis=1, concat_axis=0, tiled=True)
    by_device = jnp.broadcast_to(
        merged.reshape(row_count, chips, 1, cores * feat), (row_count, chips, cores, cores * feat)
    ).reshape(row_count, blocks, cores * feat)
    chip_rows = lax.all_to_all(by_device, BLK, split_axis=1, concat_axis=0, tiled=True).reshape(
        blocks * row_count, cores * feat
    )
    partial = jnp.dot(chip_rows, chip_weights, preferred_element_type=jnp.float32).astype(jnp.bfloat16)
    projected = lax.psum_scatter(partial, "chip", scatter_dimension=0, tiled=True).astype(jnp.float32)
    pair_rows = cores * row_count
    rows = chip_index * pair_rows + jnp.arange(pair_rows, dtype=jnp.int32)
    my_rows_img = jnp.sum((rows[:, None] >= ends[None, :]).astype(jnp.int32), axis=1)
    nimg = image_rows.shape[0]
    member = (my_rows_img[:, None] == jnp.arange(nimg, dtype=jnp.int32)[None, :]).astype(
        jnp.float32
    )
    row_squares = jnp.sum(projected * projected, axis=1)
    local_sums = jnp.sum(member * row_squares[:, None], axis=0)
    spread = jnp.broadcast_to(local_sums[None, :], (blocks, nimg))
    image_sums = jnp.sum(lax.all_to_all(spread, BLK, split_axis=0, concat_axis=0, tiled=True), axis=0)
    image_mean = image_sums / (image_rows.astype(jnp.float32) * out_width)
    row_scale = jnp.sum(member * lax.rsqrt(image_mean + 1e-06)[None, :], axis=1)
    my_gain = lax.dynamic_slice_in_dim(out_gain, core_index * half, half)
    scaled = (projected * row_scale[:, None] * my_gain[None, :]).astype(jnp.bfloat16)
    capacity = max(2, 2 * row_count // blocks)
    owner = jnp.where(
        core_index == 0,
        jnp.stack([owners[:, 0], owner_from_right]),
        jnp.stack([owner_from_left, owners[:, 0]]),
    )
    onehot = (owner[:, :, None] == jnp.arange(blocks, dtype=jnp.int32)[None, None, :]).astype(jnp.int32)
    rank = jnp.sum(jnp.cumsum(onehot, axis=1) * onehot, axis=2) - 1
    slot = (
        owner * (cores * capacity)
        + jnp.arange(cores, dtype=jnp.int32)[:, None] * capacity
        + rank
    ).reshape(pair_rows)
    placement = (
        jnp.arange(blocks * cores * capacity, dtype=jnp.int32)[:, None] == slot[None, :]
    ).astype(jnp.bfloat16)
    outgoing = jnp.dot(placement, scaled, preferred_element_type=jnp.float32).astype(jnp.bfloat16)
    incoming = lax.all_to_all(outgoing, BLK, split_axis=0, concat_axis=0, tiled=True)
    return (
        incoming.reshape(chips, cores, cores, capacity, half)
        .transpose(0, 2, 3, 1, 4)
        .reshape(blocks * capacity, out_width)
    )


def solution(mesh):
    devices = mesh.devices
    cores = 2
    split_mesh = jax.sharding.Mesh(
        devices.reshape(devices.shape[0], devices.shape[1] // cores, cores), ("dp", "chip", "core")
    )
    rows = P(("dp", "chip", "core"), None)
    in_specs = (rows, rows, rows, rows, P(), P(), P(("chip", "core"), None), P(), P("dp"), rows)
    return jax.shard_map(on_device, mesh=split_mesh, in_specs=in_specs, out_specs=rows, check_vma=False)
```

```python
import jax
import jax.numpy as jnp
from jax import lax
from jax.sharding import PartitionSpec as P

HEADS = 16


BLK = ("chip", "core")


def passed_along(value, axis, steps):
    count = lax.axis_size("chip") * lax.axis_size("core")
    first, last = (max(0, -steps), min(count, count - steps))
    return lax.ppermute(value, axis, [(source, source + steps) for source in range(first, last)])


def layer_norm(stream, gain):
    mean = jnp.mean(stream, axis=1, keepdims=True)
    centred = stream - mean
    var = jnp.mean(centred * centred, axis=1, keepdims=True)
    return centred * lax.rsqrt(var + 1e-06) * gain[None, :]


def on_device(
    queries, keys, values, residual_in, out_proj, ln_gain, merge_proj, out_gain, image_rows, owners
):
    chips = lax.axis_size("chip")
    cores = lax.axis_size("core")
    blocks = chips * cores
    me_index = lax.axis_index("chip") * cores + lax.axis_index("core")
    tok, width = queries.shape
    row_count = tok // 4
    heads = HEADS
    hdim = width // heads
    reach = min(6, (blocks - 1) // 2)
    scale = 1.0 / hdim**0.5
    ends = jnp.cumsum(image_rows)

    def token_images(source):
        rows = source * row_count + jnp.arange(tok, dtype=jnp.int32) // 4
        found = jnp.sum((rows[:, None] >= ends[None, :]).astype(jnp.int32), axis=1)
        inside = jnp.logical_and(source >= 0, source < blocks)
        return jnp.where(inside, found, -1)

    query_img = token_images(me_index)
    q_heads = queries.reshape(tok, heads, hdim)
    own_pair = jnp.stack([keys, values])

    def masked_scores(pair, key_img):
        k_heads = pair[0].reshape(-1, heads, hdim)
        scores = (
            jnp.einsum("qhd,khd->hqk", q_heads, k_heads, preferred_element_type=jnp.float32) * scale
        )
        return jnp.where(query_img[None, :, None] == key_img[None, None, :], scores, -jnp.inf)

    def weigh_values(weights, pair):
        v_heads = pair[1].reshape(-1, heads, hdim)
        return jnp.einsum(
            "hqk,khd->hqd",
            weights.astype(jnp.bfloat16),
            v_heads,
            preferred_element_type=jnp.float32,
        )

    def absorb(state, pair, key_img):

        def update(carry):
            running_max, running_sum, accum = carry
            scores = masked_scores(pair, key_img)
            new_max = jnp.maximum(running_max, jnp.max(scores, axis=2, keepdims=True))
            factor = jnp.exp(running_max - new_max)
            weights = jnp.exp(scores - new_max)
            new_sum = running_sum * factor + jnp.sum(weights, axis=2, keepdims=True)
            new_accum = accum * factor + weigh_values(weights, pair)
            return (new_max, new_sum, new_accum)

        live = jnp.logical_and(
            jnp.max(key_img) >= jnp.maximum(jnp.min(query_img), 0),
            jnp.min(jnp.where(key_img >= 0, key_img, 1 << 30)) <= jnp.max(query_img),
        )
        return lax.cond(live, update, lambda carry: carry, state)

    first_scores = masked_scores(own_pair, query_img)
    first_max = jnp.max(first_scores, axis=2, keepdims=True)
    first_weights = jnp.exp(first_scores - first_max)
    state = (
        first_max,
        jnp.sum(first_weights, axis=2, keepdims=True),
        weigh_values(first_weights, own_pair),
    )
    from_left = own_pair
    from_right = own_pair
    for step in range(1, reach + 1):
        from_left = passed_along(from_left, BLK, 1)
        from_right = passed_along(from_right, BLK, -1)
        state = absorb(state, from_left, token_images(me_index - step))
        state = absorb(state, from_right, token_images(me_index + step))
    heads_out = state[2] / state[1]
    attended = heads_out.transpose(1, 0, 2).reshape(tok, width).astype(jnp.bfloat16)
    stream = residual_in.astype(jnp.float32) + jnp.dot(
        attended, out_proj, preferred_element_type=jnp.float32
    )
    normed = layer_norm(stream, ln_gain).astype(jnp.bfloat16)
    merged = normed.reshape(row_count, 4 * width)
    feat = merge_proj.shape[0]
    out_width = merge_proj.shape[1]
    half = out_width // cores
    core_index = lax.axis_index("core")
    chip_index = lax.axis_index("chip")
    chip_weights = lax.all_to_all(merge_proj, "core", split_axis=1, concat_axis=0, tiled=True)
    by_device = jnp.broadcast_to(
        merged.reshape(row_count, chips, 1, cores * feat), (row_count, chips, cores, cores * feat)
    ).reshape(row_count, blocks, cores * feat)
    chip_rows = lax.all_to_all(by_device, BLK, split_axis=1, concat_axis=0, tiled=True).reshape(
        blocks * row_count, cores * feat
    )
    partial = jnp.dot(chip_rows, chip_weights, preferred_element_type=jnp.float32).astype(jnp.bfloat16)
    split = partial.shape[1] // 2
    first = lax.psum_scatter(partial[:, :split], "chip", scatter_dimension=0, tiled=True)
    second = jnp.sum(
        lax.all_to_all(
            partial[:, split:].reshape(chips, -1, split), "chip", split_axis=0, concat_axis=0, tiled=True
        ).astype(jnp.float32),
        axis=0,
    )
    projected = jnp.concatenate([first.astype(jnp.float32), second], axis=1)
    pair_rows = cores * row_count
    rows = chip_index * pair_rows + jnp.arange(pair_rows, dtype=jnp.int32)
    my_rows_img = jnp.sum((rows[:, None] >= ends[None, :]).astype(jnp.int32), axis=1)
    nimg = image_rows.shape[0]
    member = (my_rows_img[:, None] == jnp.arange(nimg, dtype=jnp.int32)[None, :]).astype(
        jnp.float32
    )
    row_squares = jnp.sum(projected * projected, axis=1)
    local_sums = jnp.sum(member * row_squares[:, None], axis=0)
    spread = jnp.broadcast_to(local_sums[None, :], (blocks, nimg))
    image_sums = jnp.sum(lax.all_to_all(spread, BLK, split_axis=0, concat_axis=0, tiled=True), axis=0)
    image_mean = image_sums / (image_rows.astype(jnp.float32) * out_width)
    row_scale = jnp.sum(member * lax.rsqrt(image_mean + 1e-06)[None, :], axis=1)
    my_gain = lax.dynamic_slice_in_dim(out_gain, core_index * half, half)
    scaled = (projected * row_scale[:, None] * my_gain[None, :]).astype(jnp.bfloat16)
    capacity = max(2, 2 * row_count // blocks)
    owner = lax.all_to_all(
        jnp.broadcast_to(owners[:, 0][None, :], (cores, row_count)),
        "core",
        split_axis=0,
        concat_axis=0,
        tiled=True,
    )
    onehot = (owner[:, :, None] == jnp.arange(blocks, dtype=jnp.int32)[None, None, :]).astype(jnp.int32)
    rank = jnp.sum(jnp.cumsum(onehot, axis=1) * onehot, axis=2) - 1
    slot = (
        owner * (cores * capacity)
        + jnp.arange(cores, dtype=jnp.int32)[:, None] * capacity
        + rank
    ).reshape(pair_rows)
    placement = (
        jnp.arange(blocks * cores * capacity, dtype=jnp.int32)[:, None] == slot[None, :]
    ).astype(jnp.bfloat16)
    outgoing = jnp.dot(placement, scaled, preferred_element_type=jnp.float32).astype(jnp.bfloat16)
    incoming = lax.all_to_all(outgoing, BLK, split_axis=0, concat_axis=0, tiled=True)
    return (
        incoming.reshape(chips, cores, cores, capacity, half)
        .transpose(0, 2, 3, 1, 4)
        .reshape(blocks * capacity, out_width)
    )


def solution(mesh):
    devices = mesh.devices
    cores = 2
    split_mesh = jax.sharding.Mesh(
        devices.reshape(devices.shape[0], devices.shape[1] // cores, cores), ("dp", "chip", "core")
    )
    rows = P(("dp", "chip", "core"), None)
    in_specs = (rows, rows, rows, rows, P(), P(), P(("chip", "core"), None), P(), P("dp"), rows)
    return jax.shard_map(on_device, mesh=split_mesh, in_specs=in_specs, out_specs=rows, check_vma=False)
```
